128 devices in a mesh: req: 32 (over z, x, core), seq: 4 (over y).
Axes of the slice: x: 4, y: 4, z: 4, core: 2. Of those that a mesh axis runs over, the one named last changes fastest.
Arguments:
- x_in: bfloat16 [65536, 2560], P(('req', 'seq')), may hold values from -6 to 6
- bc_in: bfloat16 [65536, 256], P(('req', 'seq')), may hold values from -6 to 6
- z_in: bfloat16 [65536, 2560], P(('req', 'seq')), may hold values from -6 to 6
- dt_raw: bfloat16 [65536, 40], P(('req', 'seq')), may hold values from -3 to 22
- conv_weight: float32 [4, 2816], replicated, may hold values from -3 to 3
- conv_bias: float32 [2816], replicated, may hold values from -0.5 to 0.5
- dt_bias: float32 [40], replicated, may hold values from -5 to -4
- a_log: float32 [40], replicated, may hold values from -3.95 to 1.17
- d_skip: float32 [40], replicated, may hold values from 0.5 to 2
- norm_gain: float32 [2560], replicated, may hold values from 0.1 to 1.9
- w_out: bfloat16 [2560, 2560], replicated, may hold values from -0.125 to 0.125
- prompt_stretches: int32 [64], replicated, may hold values from 1 to 16, as said below
Outputs:
- mixed_out: bfloat16 [65536, 2560], P(('req', 'seq'))
- end_states: float32 [256, 40, 64, 128], P('req', 'seq')
The draws below stay inside these ranges and needn't reach their ends.
Inputs may be any that keep to these rules, and one draw needn't show every extreme that they name: `prompt_stretches`: the lengths sum to 256; the last prompt is exactly 16 stretches long and none is longer.
All inputs are finite; a program needn't handle non-finite values.
Results may differ from the reference program's by a relative error of at most 0.0073.
Values may be sent and summed in bfloat16 or wider, within the bound.
No kernel may reach another device: no remote copies, remote signals or barrier semaphores. Data moves between devices by JAX's collectives and lax.ppermute only.
A program may use at most 448 MiB of HBM per device.

```python
import math
import jax
import jax.numpy as jnp
from jax import lax

D = 2560
H = 40
N = 128
KCONV = 4
STRETCH = 256
LMAX_CH = 16
TOK_DEV = 512
DI = 2560
TOKEN_TOTAL = 65536
STRETCHES = 256
REQS = 64
N_REQ = 32
N_SEQ = 4


def draw_dt_raw(key, part):
    base_random_key, flurry_random_key, height_random_key = jax.random.split(key, 3)
    base_value_rows = jnp.clip(0.5 * jax.random.normal(base_random_key, (TOKEN_TOTAL, H), jnp.float32), -3.0, 3.0)
    flurry_lengths = jax.random.uniform(flurry_random_key, (TOKEN_TOTAL, 1), jnp.float32) < 1.0 / 1024.0
    column_height = jax.random.uniform(height_random_key, (TOKEN_TOTAL, 1), jnp.float32, 17.0, 22.0)
    return jnp.where(flurry_lengths, column_height, base_value_rows).astype(jnp.bfloat16)


def draw_a_log(key, part):
    pick_key, slow_key, fast_key = jax.random.split(key, 3)
    fast_share = 0.5
    is_fast = jax.random.uniform(pick_key, (H,), jnp.float32) < fast_share
    slow_rate = jnp.exp(jax.random.uniform(slow_key, (H,), jnp.float32, math.log(0.02), math.log(0.04)))
    fast_rate = jnp.exp(jax.random.uniform(fast_key, (H,), jnp.float32, math.log(1.8), math.log(3.2)))
    return jnp.log(jnp.where(is_fast, fast_rate, slow_rate))


def draw_prompt_stretches(key, part):
    level_key, noise_key = jax.random.split(jax.random.fold_in(key, 7), 2)
    others = REQS - 1
    room = LMAX_CH - 1
    extra = STRETCHES - LMAX_CH - others
    level = jax.random.randint(level_key, (others,), 0, 16, jnp.int32)
    favour = level * level
    noise = jax.random.randint(noise_key, (others, room), 0, 256, jnp.int32)
    slot_ids = jnp.arange(others * room, dtype=jnp.int32).reshape(others, room)
    scores = (favour[:, None] + noise) * (others * room) + slot_ids
    order = jnp.argsort(-scores.reshape(-1), stable=True).astype(jnp.int32)
    ranks = jnp.argsort(order, stable=True).astype(jnp.int32).reshape(others, room)
    taken = (ranks < extra).astype(jnp.int32)
    lengths = 1 + jnp.sum(taken, axis=1).astype(jnp.int32)
    return jnp.concatenate([lengths, jnp.full((1,), LMAX_CH, jnp.int32)]).astype(jnp.int32)


def steps_of(stream_key, shape, pieces, low, largest):
    level, own = 1.0, jax.random.fold_in(stream_key, 6)
    for dim, parts in pieces:
        heights = jnp.exp(jax.random.uniform(jax.random.fold_in(own, dim), (parts,), jnp.float32, low / len(pieces), largest / len(pieces)))
        level = level * jnp.repeat(heights, shape[dim] // parts).reshape([-1 if axis == dim else 1 for axis in range(len(shape))])
    return level


def gaussian(key, dims, spread, most, cuts=(), kind=jnp.bfloat16):
    factor_of = steps_of(key, dims, cuts, -0.22, 0.18) if cuts else 1.0
    values = jax.random.normal(key, dims, jnp.float32) * spread * factor_of
    return jnp.minimum(jnp.maximum(values, -most), most).astype(kind)


def setup_inputs(seed: int = 0) -> dict:
    streams_of = jax.random.split(jax.random.key(seed), 13)
    return {
        "x_in": gaussian(streams_of[0], (TOKEN_TOTAL, DI), 1.0, 6.0, ((0, 128),)),
        "bc_in": gaussian(streams_of[1], (TOKEN_TOTAL, 2 * N), 1.0, 6.0, ((0, 128),)),
        "z_in": gaussian(streams_of[2], (TOKEN_TOTAL, DI), 1.0, 6.0, ((0, 128),)),
        "dt_raw": draw_dt_raw(jax.random.fold_in(streams_of[12], 71), 0),
        "conv_weight": gaussian(streams_of[4], (KCONV, DI + 2 * N), KCONV ** -0.5, 3.0, (), jnp.float32),
        "conv_bias": jnp.clip(jax.random.uniform(streams_of[5], (DI + 2 * N,), jnp.float32, -0.5, 0.5), -0.5, 0.5),
        "dt_bias": jnp.clip(jax.random.uniform(streams_of[6], (H,), jnp.float32, -5.0, -4.0), -5.0, -4.0),
        "a_log": draw_a_log(jax.random.fold_in(streams_of[12], 71), 0),
        "d_skip": jnp.clip(jax.random.uniform(streams_of[8], (H,), jnp.float32, 0.5, 2.0), 0.5, 2.0),
        "norm_gain": jnp.clip(1.0 + 0.18 * jax.random.normal(streams_of[9], (DI,), jnp.float32), 0.1, 1.9),
        "w_out": gaussian(streams_of[10], (DI, D), DI ** -0.5, 0.125),
        "prompt_stretches": draw_prompt_stretches(jax.random.fold_in(streams_of[12], 71), 0),
    }


def reorder_rows(token_rows):
    blocks = token_rows.reshape(N_REQ, N_SEQ, N_REQ, TOK_DEV // N_REQ, -1)
    return blocks.transpose(2, 1, 0, 3, 4).reshape(TOKEN_TOTAL, -1)

def stretch_flags(prompt_stretches, stretch_ids):
    lengths = prompt_stretches.astype(jnp.int32)
    firsts = (jnp.cumsum(lengths) - lengths).astype(jnp.int32)
    last_stretches = (firsts + lengths - 1).astype(jnp.int32)
    starts = jnp.any(stretch_ids[:, None] == firsts[None, :], axis=1)
    finals = jnp.any(stretch_ids[:, None] == last_stretches[None, :], axis=1)
    return (starts, finals)

def conv_stretch(row_block, history, weight, conv_bias):
    conv_span = weight.shape[0]
    length = row_block.shape[0]
    extended = jnp.concatenate([history, row_block], axis=0).astype(jnp.float32)
    running = conv_bias[None, :]
    for offset in range(conv_span):
        running = running + weight[offset][None, :] * extended[offset:offset + length]
    return jax.nn.silu(running).astype(jnp.bfloat16)

def local_stretch(x_stretch, bc_stretch, dt_stretch, dt_bias, a_log):
    state_size = bc_stretch.shape[1] // 2
    b_mat = bc_stretch[:, :state_size]
    c_mat = bc_stretch[:, state_size:]
    step_size = jax.nn.softplus(dt_stretch.astype(jnp.float32) + dt_bias[None, :])
    log_decay = jnp.cumsum(-jnp.exp(a_log)[None, :] * step_size, axis=0)
    scores = jnp.dot(c_mat, b_mat.T, preferred_element_type=jnp.float32)
    stretch_len = scores.shape[0]
    causal = jnp.arange(stretch_len)[:, None] >= jnp.arange(stretch_len)[None, :]
    by_head = log_decay.T
    segment = by_head[:, :, None] - by_head[:, None, :]
    decay_mask = jnp.where(causal[None], jnp.exp(jnp.where(causal[None], segment, 0.0)), 0.0)
    mixing = (scores[None] * decay_mask * step_size.T[:, None, :]).astype(jnp.bfloat16)
    y_diag = jnp.einsum('htu,uhp->thp', mixing.astype(jnp.float32), x_stretch.astype(jnp.float32))
    tail_weight = jnp.exp(log_decay[-1][None, :] - log_decay) * step_size
    weighted_x = (x_stretch.astype(jnp.float32) * tail_weight[:, :, None]).astype(jnp.bfloat16)
    stretch_state = jnp.einsum('uhp,un->hpn', weighted_x.astype(jnp.float32), b_mat.astype(jnp.float32), precision=lax.Precision.HIGHEST)
    return (y_diag, stretch_state, log_decay)

def finish_stretch(y_diag, log_decay, state_in, x_stretch, c_mat, z_stretch, d_skip, norm_gain):
    state_low = state_in.astype(jnp.bfloat16)
    y_off = jnp.exp(log_decay)[:, :, None] * jnp.einsum('tn,hpn->thp', c_mat.astype(jnp.float32), state_low.astype(jnp.float32), precision=lax.Precision.HIGHEST)
    mixed_rows = y_diag + y_off + d_skip[None, :, None] * x_stretch.astype(jnp.float32)
    mixed_rows = mixed_rows.reshape(mixed_rows.shape[0], -1)
    gated_rows = mixed_rows * jax.nn.silu(z_stretch.astype(jnp.float32))
    inv_rms = lax.rsqrt(lax.optimization_barrier(jnp.mean(gated_rows * gated_rows, axis=-1, keepdims=True)) + 1e-05)
    return (gated_rows * inv_rms * norm_gain[None, :]).astype(jnp.bfloat16)

def reference(x_in, bc_in, z_in, dt_raw, conv_weight, conv_bias, dt_bias, a_log, d_skip, norm_gain, w_out, prompt_stretches):
    inner_width = x_in.shape[1]
    head_count = a_log.shape[0]
    head_dim = inner_width // head_count
    conv_span = conv_weight.shape[0]
    x_rows = reorder_rows(x_in).reshape(STRETCHES, STRETCH, inner_width)
    bc_rows = reorder_rows(bc_in).reshape(STRETCHES, STRETCH, 2 * N)
    z_rows = reorder_rows(z_in).reshape(STRETCHES, STRETCH, inner_width)
    dt_rows = reorder_rows(dt_raw).reshape(STRETCHES, STRETCH, head_count)
    starts, finals = stretch_flags(prompt_stretches, jnp.arange(STRETCHES, dtype=jnp.int32))

    def advance(carried, element):
        state_now, hist_x, hist_bc = carried
        x_stretch, bc_stretch, z_stretch, dt_stretch, is_start, is_final = element
        hist_x = jnp.where(is_start, jnp.zeros_like(hist_x), hist_x)
        hist_bc = jnp.where(is_start, jnp.zeros_like(hist_bc), hist_bc)
        conv_x = conv_stretch(x_stretch, hist_x, conv_weight[:, :inner_width], conv_bias[:inner_width])
        conv_bc = conv_stretch(bc_stretch, hist_bc, conv_weight[:, inner_width:], conv_bias[inner_width:])
        x_heads = conv_x.reshape(STRETCH, head_count, head_dim)
        y_diag, stretch_state, log_decay = local_stretch(x_heads, conv_bc, dt_stretch, dt_bias, a_log)
        state_in = jnp.where(is_start, jnp.zeros_like(state_now), state_now)
        normed = finish_stretch(y_diag, log_decay, state_in, x_heads, conv_bc[:, N:], z_stretch, d_skip, norm_gain)
        projected = jnp.dot(normed, w_out, preferred_element_type=jnp.float32).astype(jnp.bfloat16)
        state_out = jnp.exp(log_decay[-1])[:, None, None] * state_in + stretch_state
        ending = jnp.where(is_final, state_out, jnp.zeros_like(state_out))
        return ((state_out, x_stretch[STRETCH - conv_span + 1:], bc_stretch[STRETCH - conv_span + 1:]), (projected, ending))
    initial = (jnp.zeros((head_count, head_dim, N), jnp.float32), jnp.zeros((conv_span - 1, inner_width), jnp.bfloat16), jnp.zeros((conv_span - 1, 2 * N), jnp.bfloat16))
    final_carry, outputs = lax.scan(advance, initial, (x_rows, bc_rows, z_rows, dt_rows, starts, finals))
    projected, endings = outputs
    mixed_out = reorder_rows(projected.reshape(TOKEN_TOTAL, -1))
    return (mixed_out, endings)
```

```python
import jax
import jax.numpy as jnp
from jax import lax
from jax.sharding import PartitionSpec as P

N = 128
STRETCH = 256


def from_behind(value, axis, steps):
    count = lax.axis_size(axis)
    leading, last = (max(0, -steps), min(count, count - steps))
    return lax.ppermute(value, axis, [(source, source + steps) for source in range(leading, last)])


LMAX_CH = 16


def carried_in(part, axis, combine, window):
    first = min(4, window)
    pieces = [from_behind(part, axis, k) for k in range(1, first + 1)]
    state = pieces[-1]
    for piece in reversed(pieces[:-1]):
        state = combine(state, piece)
    cover = first
    while cover < window:
        state = combine(from_behind(state, axis, cover), state)
        cover *= 2
    return state


def stretch_flags(prompt_stretches, stretch_ids):
    firsts = jnp.cumsum(prompt_stretches) - prompt_stretches
    last_stretches = firsts + prompt_stretches - 1
    starts = jnp.any(stretch_ids[:, None] == firsts[None, :], axis=1)
    finals = jnp.any(stretch_ids[:, None] == last_stretches[None, :], axis=1)
    return (starts, finals)


def causal_conv(row_block, history, weight, conv_bias, starts):
    conv_span = weight.shape[0]
    length = row_block.shape[0]
    extended = jnp.concatenate([history, row_block], axis=0)
    in_stretch = jnp.arange(length, dtype=jnp.int32) % STRETCH
    start_rows = jnp.repeat(starts, STRETCH)
    running = conv_bias[None, :]
    for offset in range(conv_span):
        lag_rows = conv_span - 1 - offset
        shifted = extended[offset : offset + length].astype(jnp.float32)
        usable = jnp.logical_not((in_stretch < lag_rows) & start_rows)
        running = running + weight[offset][None, :] * jnp.where(usable[:, None], shifted, 0.0)
    return jax.nn.silu(running).astype(jnp.bfloat16)


def local_stretch(x_stretch, bc_stretch, dt_stretch, dt_bias, a_log):
    state_size = bc_stretch.shape[1] // 2
    b_mat = bc_stretch[:, :state_size]
    c_mat = bc_stretch[:, state_size:]
    step_size = jax.nn.softplus(dt_stretch.astype(jnp.float32) + dt_bias[None, :])
    log_decay = jnp.cumsum(-jnp.exp(a_log)[None, :] * step_size, axis=0)
    scores = jnp.dot(c_mat, b_mat.T, preferred_element_type=jnp.float32)
    stretch_len = scores.shape[0]
    causal = jnp.arange(stretch_len)[:, None] >= jnp.arange(stretch_len)[None, :]
    by_head = log_decay.T
    segment = by_head[:, :, None] - by_head[:, None, :]
    decay_mask = jnp.where(causal[None], jnp.exp(jnp.where(causal[None], segment, 0.0)), 0.0)
    mixing = (scores[None] * decay_mask * step_size.T[:, None, :]).astype(jnp.bfloat16)
    y_diag = jnp.einsum("htu,uhp->thp", mixing, x_stretch, preferred_element_type=jnp.float32)
    tail_weight = jnp.exp(log_decay[-1][None, :] - log_decay) * step_size
    weighted_x = (x_stretch.astype(jnp.float32) * tail_weight[:, :, None]).astype(jnp.bfloat16)
    stretch_state = jnp.einsum("uhp,un->hpn", weighted_x, b_mat, preferred_element_type=jnp.float32)
    return (y_diag, stretch_state, log_decay)


def finish_stretch(y_diag, log_decay, state_in, x_stretch, c_mat, z_stretch, d_skip, norm_gain):
    state_low = state_in.astype(jnp.bfloat16)
    y_off = jnp.exp(log_decay)[:, :, None] * jnp.einsum(
        "tn,hpn->thp", c_mat, state_low, preferred_element_type=jnp.float32
    )
    mixed_rows = y_diag + y_off + d_skip[None, :, None] * x_stretch.astype(jnp.float32)
    mixed_rows = mixed_rows.reshape(mixed_rows.shape[0], -1)
    gated_rows = mixed_rows * jax.nn.silu(z_stretch.astype(jnp.float32))
    inv_rms = lax.rsqrt(jnp.mean(gated_rows * gated_rows, axis=-1, keepdims=True) + 1e-05)
    return (gated_rows * inv_rms * norm_gain[None, :]).astype(jnp.bfloat16)


def chain_states(earlier, later):
    return (earlier[0] * later[0], later[0][:, None, None] * earlier[1] + later[1])


def per_device(
    x_in,
    bc_in,
    z_in,
    dt_raw,
    conv_weight,
    conv_bias,
    dt_bias,
    a_log,
    d_skip,
    norm_gain,
    w_out,
    prompt_stretches,
):
    x_rows, bc_rows, z_rows, dt_rows = (
        lax.all_to_all(x_in, "req", split_axis=0, concat_axis=0, tiled=True),
        lax.all_to_all(bc_in, "req", split_axis=0, concat_axis=0, tiled=True),
        lax.all_to_all(z_in, "req", split_axis=0, concat_axis=0, tiled=True),
        lax.all_to_all(dt_raw, "req", split_axis=0, concat_axis=0, tiled=True),
    )
    row_count = x_rows.shape[0]
    inner_width = x_rows.shape[1]
    head_count = a_log.shape[0]
    head_dim = inner_width // head_count
    stretch_count = row_count // STRETCH
    conv_span = conv_weight.shape[0]
    device = lax.axis_index(("req", "seq"))
    stretch_ids = device * stretch_count + jnp.arange(stretch_count, dtype=jnp.int32)
    starts, finals = stretch_flags(prompt_stretches, stretch_ids)
    edge_x, edge_bc = from_behind(
        (x_rows[row_count - conv_span + 1 :], bc_rows[row_count - conv_span + 1 :]),
        ("req", "seq"),
        1,
    )
    conv_x = causal_conv(
        x_rows, edge_x, conv_weight[:, :inner_width], conv_bias[:inner_width], starts
    )
    conv_bc = causal_conv(
        bc_rows, edge_bc, conv_weight[:, inner_width:], conv_bias[inner_width:], starts
    )
    x_heads = conv_x.reshape(stretch_count, STRETCH, head_count, head_dim)
    bc_stretches = conv_bc.reshape(stretch_count, STRETCH, 2 * N)
    dt_stretches = dt_rows.reshape(stretch_count, STRETCH, head_count)

    def stretch_work(element):
        return local_stretch(element[0], element[1], element[2], dt_bias, a_log)

    y_diag, stretch_state, log_decay = lax.map(stretch_work, (x_heads, bc_stretches, dt_stretches))
    carried = jnp.where(starts[:, None], 0.0, jnp.exp(log_decay[:, -1, :]))
    total_gain = jnp.ones((head_count,), jnp.float32)
    total_state = jnp.zeros((head_count, head_dim, N), jnp.float32)
    for stretch in range(stretch_count):
        total_gain, total_state = chain_states(
            (total_gain, total_state), (carried[stretch], stretch_state[stretch])
        )
    window = -(-(LMAX_CH - 1) // stretch_count)
    incoming = carried_in((total_gain, total_state), ("req", "seq"), chain_states, window)
    state_prev = incoming[1]
    normed_parts = []
    ending_parts = []
    for stretch in range(stretch_count):
        state_in = jnp.where(starts[stretch], jnp.zeros_like(state_prev), state_prev)
        z_stretch = z_rows[stretch * STRETCH : (stretch + 1) * STRETCH]
        normed_parts.append(
            finish_stretch(
                y_diag[stretch],
                log_decay[stretch],
                state_in,
                x_heads[stretch],
                bc_stretches[stretch, :, N:],
                z_stretch,
                d_skip,
                norm_gain,
            )
        )
        state_out = (
            jnp.exp(log_decay[stretch, -1])[:, None, None] * state_in + stretch_state[stretch]
        )
        ending_parts.append(jnp.where(finals[stretch], state_out, jnp.zeros_like(state_out)))
        state_prev = state_out
    normed = jnp.concatenate(normed_parts, axis=0)
    endings = lax.all_to_all(
        jnp.stack(ending_parts, axis=0), "seq", split_axis=1, concat_axis=0, tiled=True
    )
    projected = jnp.dot(normed, w_out, preferred_element_type=jnp.float32).astype(jnp.bfloat16)
    mixed_out = lax.all_to_all(projected, "req", split_axis=0, concat_axis=0, tiled=True)
    return (mixed_out, endings)


def solution(mesh):
    placed = (
        P(("req", "seq"), None),
        P(("req", "seq"), None),
        P(("req", "seq"), None),
        P(("req", "seq"), None),
        P(),
        P(),
        P(),
        P(),
        P(),
        P(),
        P(),
        P(),
    )
    return jax.shard_map(
        per_device,
        mesh=mesh,
        in_specs=placed,
        out_specs=(P(("req", "seq"), None), P("req", "seq", None, None)),
        check_vma=False,
    )
```

```python
import jax
import jax.numpy as jnp
from jax import lax
from jax.sharding import PartitionSpec as P

N = 128
STRETCH = 256


def from_behind(value, axis, steps):
    count = lax.axis_size(axis)
    leading, last = (max(0, -steps), min(count, count - steps))
    return lax.ppermute(value, axis, [(source, source + steps) for source in range(leading, last)])


LMAX_CH = 16


def chain_flat(earlier, later):
    return (earlier[0] * later[0], later[0][:, None] * earlier[1] + later[1])


def carried_in(gain, state, window):
    groups = lax.axis_size("seq")
    heads = gain.shape[0]
    share = heads // groups
    cells = state.shape[1] * state.shape[2]
    packed = jnp.concatenate(
        [state.reshape(heads, cells), jnp.broadcast_to(gain[:, None], (heads, 128))], axis=1
    )
    mine = lax.all_to_all(packed, "seq", split_axis=0, concat_axis=0, tiled=True)
    mine = mine.reshape(groups, share, cells + 128)
    parts = [(mine[k, :, cells], mine[k, :, :cells]) for k in range(groups)]
    prefixes = [(jnp.ones((share,), jnp.float32), jnp.zeros((share, cells), jnp.float32))]
    for k in range(groups):
        prefixes.append(chain_flat(prefixes[-1], parts[k]))
    whole = prefixes[-1]
    reach = -(-window // groups)
    behind = from_behind(whole, "req", reach)
    for step in range(reach - 1, 0, -1):
        behind = chain_flat(behind, from_behind(whole, "req", step))
    incoming = jnp.stack([chain_flat(behind, prefixes[k])[1] for k in range(groups)], axis=0)
    incoming = lax.all_to_all(incoming, "seq", split_axis=0, concat_axis=0, tiled=True)
    return incoming.reshape(state.shape)


def stretch_flags(prompt_stretches, stretch_ids):
    firsts = jnp.cumsum(prompt_stretches) - prompt_stretches
    last_stretches = firsts + prompt_stretches - 1
    starts = jnp.any(stretch_ids[:, None] == firsts[None, :], axis=1)
    finals = jnp.any(stretch_ids[:, None] == last_stretches[None, :], axis=1)
    return (starts, finals)


def causal_conv(row_block, history, weight, conv_bias, starts):
    conv_span = weight.shape[0]
    length = row_block.shape[0]
    extended = jnp.concatenate([history, row_block], axis=0)
    in_stretch = jnp.arange(length, dtype=jnp.int32) % STRETCH
    start_rows = jnp.repeat(starts, STRETCH)
    running = conv_bias[None, :]
    for offset in range(conv_span):
        lag_rows = conv_span - 1 - offset
        shifted = extended[offset : offset + length].astype(jnp.float32)
        usable = jnp.logical_not((in_stretch < lag_rows) & start_rows)
        running = running + weight[offset][None, :] * jnp.where(usable[:, None], shifted, 0.0)
    return jax.nn.silu(running).astype(jnp.bfloat16)


def local_stretch(x_stretch, bc_stretch, dt_stretch, dt_bias, a_log):
    state_size = bc_stretch.shape[1] // 2
    b_mat = bc_stretch[:, :state_size]
    c_mat = bc_stretch[:, state_size:]
    step_size = jax.nn.softplus(dt_stretch.astype(jnp.float32) + dt_bias[None, :])
    log_decay = jnp.cumsum(-jnp.exp(a_log)[None, :] * step_size, axis=0)
    scores = jnp.dot(c_mat, b_mat.T, preferred_element_type=jnp.float32)
    stretch_len = scores.shape[0]
    causal = jnp.arange(stretch_len)[:, None] >= jnp.arange(stretch_len)[None, :]
    by_head = log_decay.T
    segment = by_head[:, :, None] - by_head[:, None, :]
    decay_mask = jnp.where(causal[None], jnp.exp(jnp.where(causal[None], segment, 0.0)), 0.0)
    mixing = (scores[None] * decay_mask * step_size.T[:, None, :]).astype(jnp.bfloat16)
    y_diag = jnp.einsum("htu,uhp->thp", mixing, x_stretch, preferred_element_type=jnp.float32)
    tail_weight = jnp.exp(log_decay[-1][None, :] - log_decay) * step_size
    weighted_x = (x_stretch.astype(jnp.float32) * tail_weight[:, :, None]).astype(jnp.bfloat16)
    stretch_state = jnp.einsum("uhp,un->hpn", weighted_x, b_mat, preferred_element_type=jnp.float32)
    return (y_diag, stretch_state, log_decay)


def finish_stretch(y_diag, log_decay, state_in, x_stretch, c_mat, z_stretch, d_skip, norm_gain):
    state_low = state_in.astype(jnp.bfloat16)
    y_off = jnp.exp(log_decay)[:, :, None] * jnp.einsum(
        "tn,hpn->thp", c_mat, state_low, preferred_element_type=jnp.float32
    )
    mixed_rows = y_diag + y_off + d_skip[None, :, None] * x_stretch.astype(jnp.float32)
    mixed_rows = mixed_rows.reshape(mixed_rows.shape[0], -1)
    gated_rows = mixed_rows * jax.nn.silu(z_stretch.astype(jnp.float32))
    inv_rms = lax.rsqrt(jnp.mean(gated_rows * gated_rows, axis=-1, keepdims=True) + 1e-05)
    return (gated_rows * inv_rms * norm_gain[None, :]).astype(jnp.bfloat16)


def chain_states(earlier, later):
    return (earlier[0] * later[0], later[0][:, None, None] * earlier[1] + later[1])


def per_device(
    x_in,
    bc_in,
    z_in,
    dt_raw,
    conv_weight,
    conv_bias,
    dt_bias,
    a_log,
    d_skip,
    norm_gain,
    w_out,
    prompt_stretches,
):
    x_rows, bc_rows, z_rows, dt_rows = (
        lax.all_to_all(x_in, "req", split_axis=0, concat_axis=0, tiled=True),
        lax.all_to_all(bc_in, "req", split_axis=0, concat_axis=0, tiled=True),
        lax.all_to_all(z_in, "req", split_axis=0, concat_axis=0, tiled=True),
        lax.all_to_all(dt_raw, "req", split_axis=0, concat_axis=0, tiled=True),
    )
    row_count = x_rows.shape[0]
    inner_width = x_rows.shape[1]
    head_count = a_log.shape[0]
    head_dim = inner_width // head_count
    stretch_count = row_count // STRETCH
    conv_span = conv_weight.shape[0]
    device = lax.axis_index(("req", "seq"))
    stretch_ids = device * stretch_count + jnp.arange(stretch_count, dtype=jnp.int32)
    starts, finals = stretch_flags(prompt_stretches, stretch_ids)
    edge_x, edge_bc = from_behind(
        (x_rows[row_count - conv_span + 1 :], bc_rows[row_count - conv_span + 1 :]),
        ("req", "seq"),
        1,
    )
    conv_x = causal_conv(
        x_rows, edge_x, conv_weight[:, :inner_width], conv_bias[:inner_width], starts
    )
    conv_bc = causal_conv(
        bc_rows, edge_bc, conv_weight[:, inner_width:], conv_bias[inner_width:], starts
    )
    x_heads = conv_x.reshape(stretch_count, STRETCH, head_count, head_dim)
    bc_stretches = conv_bc.reshape(stretch_count, STRETCH, 2 * N)
    dt_stretches = dt_rows.reshape(stretch_count, STRETCH, head_count)

    def stretch_work(element):
        return local_stretch(element[0], element[1], element[2], dt_bias, a_log)

    y_diag, stretch_state, log_decay = lax.map(stretch_work, (x_heads, bc_stretches, dt_stretches))
    carried = jnp.where(starts[:, None], 0.0, jnp.exp(log_decay[:, -1, :]))
    total_gain = jnp.ones((head_count,), jnp.float32)
    total_state = jnp.zeros((head_count, head_dim, N), jnp.float32)
    for stretch in range(stretch_count):
        total_gain, total_state = chain_states(
            (total_gain, total_state), (carried[stretch], stretch_state[stretch])
        )
    window = -(-(LMAX_CH - 1) // stretch_count)
    state_prev = carried_in(total_gain, total_state, window)
    normed_parts = []
    ending_parts = []
    for stretch in range(stretch_count):
        state_in = jnp.where(starts[stretch], jnp.zeros_like(state_prev), state_prev)
        z_stretch = z_rows[stretch * STRETCH : (stretch + 1) * STRETCH]
        normed_parts.append(
            finish_stretch(
                y_diag[stretch],
                log_decay[stretch],
                state_in,
                x_heads[stretch],
                bc_stretches[stretch, :, N:],
                z_stretch,
                d_skip,
                norm_gain,
            )
        )
        state_out = (
            jnp.exp(log_decay[stretch, -1])[:, None, None] * state_in + stretch_state[stretch]
        )
        ending_parts.append(jnp.where(finals[stretch], state_out, jnp.zeros_like(state_out)))
        state_prev = state_out
    normed = jnp.concatenate(normed_parts, axis=0)
    endings = lax.all_to_all(
        jnp.stack(ending_parts, axis=0), "seq", split_axis=1, concat_axis=0, tiled=True
    )
    projected = jnp.dot(normed, w_out, preferred_element_type=jnp.float32).astype(jnp.bfloat16)
    mixed_out = lax.all_to_all(projected, "req", split_axis=0, concat_axis=0, tiled=True)
    return (mixed_out, endings)


def solution(mesh):
    placed = (
        P(("req", "seq"), None),
        P(("req", "seq"), None),
        P(("req", "seq"), None),
        P(("req", "seq"), None),
        P(),
        P(),
        P(),
        P(),
        P(),
        P(),
        P(),
        P(),
    )
    return jax.shard_map(
        per_device,
        mesh=mesh,
        in_specs=placed,
        out_specs=(P(("req", "seq"), None), P("req", "seq", None, None)),
        check_vma=False,
    )
```

```python
import jax
import jax.numpy as jnp
from jax import lax
from jax.sharding import PartitionSpec as P

N = 128
STRETCH = 256


def from_behind(value, axis, steps):
    count = lax.axis_size(axis)
    leading, last = (max(0, -steps), min(count, count - steps))
    return lax.ppermute(value, axis, [(source, source + steps) for source in range(leading, last)])


LMAX_CH = 16


def chain_flat(earlier, later):
    return (earlier[0] * later[0], later[0][:, None] * earlier[1] + later[1])


def carried_in(gain, state, window):
    groups = lax.axis_size("seq")
    heads = gain.shape[0]
    share = heads // groups
    cells = state.shape[1] * state.shape[2]
    packed = jnp.concatenate(
        [state.reshape(heads, cells), jnp.broadcast_to(gain[:, None], (heads, 128))], axis=1
    )
    mine = lax.all_to_all(packed, "seq", split_axis=0, concat_axis=0, tiled=True)
    mine = mine.reshape(groups, share, cells + 128)
    parts = [(mine[k, :, cells], mine[k, :, :cells]) for k in range(groups)]
    prefixes = [(jnp.ones((share,), jnp.float32), jnp.zeros((share, cells), jnp.float32))]
    for k in range(groups):
        prefixes.append(chain_flat(prefixes[-1], parts[k]))
    whole = prefixes[-1]
    reach = -(-window // groups)
    behind = from_behind(whole, "req", reach)
    for step in range(reach - 1, 0, -1):
        behind = chain_flat(behind, from_behind(whole, "req", step))
    incoming = jnp.stack([chain_flat(behind, prefixes[k])[1] for k in range(groups)], axis=0)
    incoming = lax.all_to_all(incoming, "seq", split_axis=0, concat_axis=0, tiled=True)
    return incoming.reshape(state.shape)


def stretch_flags(prompt_stretches, stretch_ids):
    firsts = jnp.cumsum(prompt_stretches) - prompt_stretches
    last_stretches = firsts + prompt_stretches - 1
    starts = jnp.any(stretch_ids[:, None] == firsts[None, :], axis=1)
    finals = jnp.any(stretch_ids[:, None] == last_stretches[None, :], axis=1)
    return (starts, finals)


def causal_conv(row_block, history, weight, conv_bias, starts):
    conv_span = weight.shape[0]
    length = row_block.shape[0]
    extended = jnp.concatenate([history, row_block], axis=0)
    in_stretch = jnp.arange(length, dtype=jnp.int32) % STRETCH
    start_rows = jnp.repeat(starts, STRETCH)
    running = conv_bias[None, :]
    for offset in range(conv_span):
        lag_rows = conv_span - 1 - offset
        shifted = extended[offset : offset + length].astype(jnp.float32)
        usable = jnp.logical_not((in_stretch < lag_rows) & start_rows)
        running = running + weight[offset][None, :] * jnp.where(usable[:, None], shifted, 0.0)
    return jax.nn.silu(running).astype(jnp.bfloat16)


def local_stretch(x_stretch, bc_stretch, dt_stretch, dt_bias, a_log):
    state_size = bc_stretch.shape[1] // 2
    b_mat = bc_stretch[:, :state_size]
    c_mat = bc_stretch[:, state_size:]
    step_size = jax.nn.softplus(dt_stretch.astype(jnp.float32) + dt_bias[None, :])
    log_decay = jnp.cumsum(-jnp.exp(a_log)[None, :] * step_size, axis=0)
    scores = jnp.dot(c_mat, b_mat.T, preferred_element_type=jnp.float32)
    stretch_len = scores.shape[0]
    causal = jnp.arange(stretch_len)[:, None] >= jnp.arange(stretch_len)[None, :]
    by_head = log_decay.T
    segment = by_head[:, :, None] - by_head[:, None, :]
    decay_mask = jnp.where(causal[None], jnp.exp(jnp.where(causal[None], segment, 0.0)), 0.0)
    mixing = (scores[None] * decay_mask * step_size.T[:, None, :]).astype(jnp.bfloat16)
    y_diag = jnp.einsum("htu,uhp->thp", mixing, x_stretch, preferred_element_type=jnp.float32)
    tail_weight = jnp.exp(log_decay[-1][None, :] - log_decay) * step_size
    weighted_x = (x_stretch.astype(jnp.float32) * tail_weight[:, :, None]).astype(jnp.bfloat16)
    stretch_state = jnp.einsum("uhp,un->hpn", weighted_x, b_mat, preferred_element_type=jnp.float32)
    return (y_diag, stretch_state, log_decay)


def finish_stretch(y_diag, log_decay, state_in, x_stretch, c_mat, d_skip):
    state_low = state_in.astype(jnp.bfloat16)
    y_off = jnp.exp(log_decay)[:, :, None] * jnp.einsum(
        "tn,hpn->thp", c_mat, state_low, preferred_element_type=jnp.float32
    )
    mixed_rows = y_diag + y_off + d_skip[None, :, None] * x_stretch.astype(jnp.float32)
    return mixed_rows.reshape(mixed_rows.shape[0], -1).astype(jnp.bfloat16)


def gate_and_norm(mixed_rows, z_rows, norm_gain):
    gated_rows = mixed_rows.astype(jnp.float32) * jax.nn.silu(z_rows.astype(jnp.float32))
    inv_rms = lax.rsqrt(jnp.mean(gated_rows * gated_rows, axis=-1, keepdims=True) + 1e-05)
    return (gated_rows * inv_rms * norm_gain[None, :]).astype(jnp.bfloat16)


def chain_states(earlier, later):
    return (earlier[0] * later[0], later[0][:, None, None] * earlier[1] + later[1])


def per_device(
    x_in,
    bc_in,
    z_in,
    dt_raw,
    conv_weight,
    conv_bias,
    dt_bias,
    a_log,
    d_skip,
    norm_gain,
    w_out,
    prompt_stretches,
):
    inner_width = x_in.shape[1]
    bc_width = bc_in.shape[1]
    joined = lax.all_to_all(
        jnp.concatenate([x_in, bc_in, dt_raw], axis=1), "req", split_axis=0, concat_axis=0, tiled=True
    )
    x_rows = joined[:, :inner_width]
    bc_rows = joined[:, inner_width : inner_width + bc_width]
    dt_rows = joined[:, inner_width + bc_width :]
    row_count = x_rows.shape[0]
    head_count = a_log.shape[0]
    head_dim = inner_width // head_count
    stretch_count = row_count // STRETCH
    conv_span = conv_weight.shape[0]
    device = lax.axis_index(("req", "seq"))
    stretch_ids = device * stretch_count + jnp.arange(stretch_count, dtype=jnp.int32)
    starts, finals = stretch_flags(prompt_stretches, stretch_ids)
    edge_x, edge_bc = from_behind(
        (x_rows[row_count - conv_span + 1 :], bc_rows[row_count - conv_span + 1 :]),
        ("req", "seq"),
        1,
    )
    conv_x = causal_conv(
        x_rows, edge_x, conv_weight[:, :inner_width], conv_bias[:inner_width], starts
    )
    conv_bc = causal_conv(
        bc_rows, edge_bc, conv_weight[:, inner_width:], conv_bias[inner_width:], starts
    )
    x_heads = conv_x.reshape(stretch_count, STRETCH, head_count, head_dim)
    bc_stretches = conv_bc.reshape(stretch_count, STRETCH, 2 * N)
    dt_stretches = dt_rows.reshape(stretch_count, STRETCH, head_count)

    def stretch_work(element):
        return local_stretch(element[0], element[1], element[2], dt_bias, a_log)

    y_diag, stretch_state, log_decay = lax.map(stretch_work, (x_heads, bc_stretches, dt_stretches))
    carried = jnp.where(starts[:, None], 0.0, jnp.exp(log_decay[:, -1, :]))
    total_gain = jnp.ones((head_count,), jnp.float32)
    total_state = jnp.zeros((head_count, head_dim, N), jnp.float32)
    for stretch in range(stretch_count):
        total_gain, total_state = chain_states(
            (total_gain, total_state), (carried[stretch], stretch_state[stretch])
        )
    window = -(-(LMAX_CH - 1) // stretch_count)
    state_prev = carried_in(total_gain, total_state, window)
    normed_parts = []
    ending_parts = []
    for stretch in range(stretch_count):
        state_in = jnp.where(starts[stretch], jnp.zeros_like(state_prev), state_prev)
        normed_parts.append(
            finish_stretch(
                y_diag[stretch],
                log_decay[stretch],
                state_in,
                x_heads[stretch],
                bc_stretches[stretch, :, N:],
                d_skip,
            )
        )
        state_out = (
            jnp.exp(log_decay[stretch, -1])[:, None, None] * state_in + stretch_state[stretch]
        )
        ending_parts.append(jnp.where(finals[stretch], state_out, jnp.zeros_like(state_out)))
        state_prev = state_out
    mixed_stream = jnp.concatenate(normed_parts, axis=0)
    endings = lax.all_to_all(
        jnp.stack(ending_parts, axis=0), "seq", split_axis=1, concat_axis=0, tiled=True
    )
    mixed_tokens = lax.all_to_all(mixed_stream, "req", split_axis=0, concat_axis=0, tiled=True)
    normed = gate_and_norm(mixed_tokens, z_in, norm_gain)
    mixed_out = jnp.dot(normed, w_out, preferred_element_type=jnp.float32).astype(jnp.bfloat16)
    return (mixed_out, endings)


def solution(mesh):
    placed = (
        P(("req", "seq"), None),
        P(("req", "seq"), None),
        P(("req", "seq"), None),
        P(("req", "seq"), None),
        P(),
        P(),
        P(),
        P(),
        P(),
        P(),
        P(),
        P(),
    )
    return jax.shard_map(
        per_device,
        mesh=mesh,
        in_specs=placed,
        out_specs=(P(("req", "seq"), None), P("req", "seq", None, None)),
        check_vma=False,
    )
```

```python
import jax
import jax.numpy as jnp
from jax import lax
from jax.sharding import PartitionSpec as P

N = 128
STRETCH = 256


def from_behind(value, axis, steps):
    count = lax.axis_size(axis)
    leading, last = (max(0, -steps), min(count, count - steps))
    return lax.ppermute(value, axis, [(source, source + steps) for source in range(leading, last)])


LMAX_CH = 16


def chain_flat(earlier, later):
    return (earlier[0] * later[0], later[0][:, None] * earlier[1] + later[1])


def carried_in(gain, state, window):
    groups = lax.axis_size("seq")
    heads = gain.shape[0]
    share = heads // groups
    cells = state.shape[1] * state.shape[2]
    packed = jnp.concatenate(
        [state.reshape(heads, cells), jnp.broadcast_to(gain[:, None], (heads, 128))], axis=1
    )
    mine = lax.all_to_all(packed, "seq", split_axis=0, concat_axis=0, tiled=True)
    mine = mine.reshape(groups, share, cells + 128)
    parts = [(mine[k, :, cells], mine[k, :, :cells]) for k in range(groups)]
    prefixes = [(jnp.ones((share,), jnp.float32), jnp.zeros((share, cells), jnp.float32))]
    for k in range(groups):
        prefixes.append(chain_flat(prefixes[-1], parts[k]))
    whole = prefixes[-1]
    reach = -(-window // groups)
    behind = from_behind(whole, "req", reach)
    for step in range(reach - 1, 0, -1):
        behind = chain_flat(behind, from_behind(whole, "req", step))
    incoming = jnp.stack([chain_flat(behind, prefixes[k])[1] for k in range(groups)], axis=0)
    incoming = lax.all_to_all(incoming, "seq", split_axis=0, concat_axis=0, tiled=True)
    return incoming.reshape(state.shape)


def stretch_flags(prompt_stretches, stretch_ids):
    firsts = jnp.cumsum(prompt_stretches) - prompt_stretches
    last_stretches = firsts + prompt_stretches - 1
    starts = jnp.any(stretch_ids[:, None] == firsts[None, :], axis=1)
    finals = jnp.any(stretch_ids[:, None] == last_stretches[None, :], axis=1)
    return (starts, finals)


def causal_conv(row_block, history, weight, conv_bias, starts):
    conv_span = weight.shape[0]
    length = row_block.shape[0]
    extended = jnp.concatenate([history, row_block], axis=0)
    in_stretch = jnp.arange(length, dtype=jnp.int32) % STRETCH
    start_rows = jnp.repeat(starts, STRETCH)
    running = conv_bias[None, :]
    for offset in range(conv_span):
        lag_rows = conv_span - 1 - offset
        shifted = extended[offset : offset + length].astype(jnp.float32)
        usable = jnp.logical_not((in_stretch < lag_rows) & start_rows)
        running = running + weight[offset][None, :] * jnp.where(usable[:, None], shifted, 0.0)
    return jax.nn.silu(running).astype(jnp.bfloat16)


def stretch_summary(x_stretch, bc_stretch, dt_stretch, dt_bias, a_log):
    state_size = bc_stretch.shape[1] // 2
    b_mat = bc_stretch[:, :state_size]
    step_size = jax.nn.softplus(dt_stretch.astype(jnp.float32) + dt_bias[None, :])
    log_decay = jnp.cumsum(-jnp.exp(a_log)[None, :] * step_size, axis=0)
    tail_weight = jnp.exp(log_decay[-1][None, :] - log_decay) * step_size
    weighted_x = (x_stretch.astype(jnp.float32) * tail_weight[:, :, None]).astype(jnp.bfloat16)
    stretch_state = jnp.einsum("uhp,un->hpn", weighted_x, b_mat, preferred_element_type=jnp.float32)
    return (step_size, log_decay, stretch_state)


def stretch_diag(x_stretch, bc_stretch, step_size, log_decay):
    state_size = bc_stretch.shape[1] // 2
    b_mat = bc_stretch[:, :state_size]
    c_mat = bc_stretch[:, state_size:]
    scores = jnp.dot(c_mat, b_mat.T, preferred_element_type=jnp.float32)
    stretch_len = scores.shape[0]
    causal = jnp.arange(stretch_len)[:, None] >= jnp.arange(stretch_len)[None, :]
    by_head = log_decay.T
    segment = by_head[:, :, None] - by_head[:, None, :]
    decay_mask = jnp.where(causal[None], jnp.exp(jnp.where(causal[None], segment, 0.0)), 0.0)
    mixing = (scores[None] * decay_mask * step_size.T[:, None, :]).astype(jnp.bfloat16)
    return jnp.einsum("htu,uhp->thp", mixing, x_stretch, preferred_element_type=jnp.float32)


def finish_stretch(y_diag, log_decay, state_in, x_stretch, c_mat, d_skip):
    state_low = state_in.astype(jnp.bfloat16)
    y_off = jnp.exp(log_decay)[:, :, None] * jnp.einsum(
        "tn,hpn->thp", c_mat, state_low, preferred_element_type=jnp.float32
    )
    mixed_rows = y_diag + y_off + d_skip[None, :, None] * x_stretch.astype(jnp.float32)
    return mixed_rows.reshape(mixed_rows.shape[0], -1).astype(jnp.bfloat16)


def gate_and_norm(mixed_rows, z_rows, norm_gain):
    gated_rows = mixed_rows.astype(jnp.float32) * jax.nn.silu(z_rows.astype(jnp.float32))
    inv_rms = lax.rsqrt(jnp.mean(gated_rows * gated_rows, axis=-1, keepdims=True) + 1e-05)
    return (gated_rows * inv_rms * norm_gain[None, :]).astype(jnp.bfloat16)


def chain_states(earlier, later):
    return (earlier[0] * later[0], later[0][:, None, None] * earlier[1] + later[1])


def per_device(
    x_in,
    bc_in,
    z_in,
    dt_raw,
    conv_weight,
    conv_bias,
    dt_bias,
    a_log,
    d_skip,
    norm_gain,
    w_out,
    prompt_stretches,
):
    inner_width = x_in.shape[1]
    bc_width = bc_in.shape[1]
    joined = lax.all_to_all(
        jnp.concatenate([x_in, bc_in, dt_raw], axis=1), "req", split_axis=0, concat_axis=0, tiled=True
    )
    x_rows = joined[:, :inner_width]
    bc_rows = joined[:, inner_width : inner_width + bc_width]
    dt_rows = joined[:, inner_width + bc_width :]
    row_count = x_rows.shape[0]
    head_count = a_log.shape[0]
    head_dim = inner_width // head_count
    stretch_count = row_count // STRETCH
    conv_span = conv_weight.shape[0]
    device = lax.axis_index(("req", "seq"))
    stretch_ids = device * stretch_count + jnp.arange(stretch_count, dtype=jnp.int32)
    starts, finals = stretch_flags(prompt_stretches, stretch_ids)
    edge_x, edge_bc = from_behind(
        (x_rows[row_count - conv_span + 1 :], bc_rows[row_count - conv_span + 1 :]),
        ("req", "seq"),
        1,
    )
    conv_x = causal_conv(
        x_rows, edge_x, conv_weight[:, :inner_width], conv_bias[:inner_width], starts
    )
    conv_bc = causal_conv(
        bc_rows, edge_bc, conv_weight[:, inner_width:], conv_bias[inner_width:], starts
    )
    x_heads = conv_x.reshape(stretch_count, STRETCH, head_count, head_dim)
    bc_stretches = conv_bc.reshape(stretch_count, STRETCH, 2 * N)
    dt_stretches = dt_rows.reshape(stretch_count, STRETCH, head_count)

    summaries = [
        stretch_summary(x_heads[c], bc_stretches[c], dt_stretches[c], dt_bias, a_log)
        for c in range(stretch_count)
    ]
    step_size = jnp.stack([s[0] for s in summaries], axis=0)
    log_decay = jnp.stack([s[1] for s in summaries], axis=0)
    stretch_state = jnp.stack([s[2] for s in summaries], axis=0)
    y_diag = [
        stretch_diag(x_heads[c], bc_stretches[c], step_size[c], log_decay[c])
        for c in range(stretch_count)
    ]
    carried = jnp.where(starts[:, None], 0.0, jnp.exp(log_decay[:, -1, :]))
    total_gain = jnp.ones((head_count,), jnp.float32)
    total_state = jnp.zeros((head_count, head_dim, N), jnp.float32)
    for stretch in range(stretch_count):
        total_gain, total_state = chain_states(
            (total_gain, total_state), (carried[stretch], stretch_state[stretch])
        )
    window = -(-(LMAX_CH - 1) // stretch_count)
    state_prev = carried_in(total_gain, total_state, window)
    normed_parts = []
    ending_parts = []
    for stretch in range(stretch_count):
        state_in = jnp.where(starts[stretch], jnp.zeros_like(state_prev), state_prev)
        normed_parts.append(
            finish_stretch(
                y_diag[stretch],
                log_decay[stretch],
                state_in,
                x_heads[stretch],
                bc_stretches[stretch, :, N:],
                d_skip,
            )
        )
        state_out = (
            jnp.exp(log_decay[stretch, -1])[:, None, None] * state_in + stretch_state[stretch]
        )
        ending_parts.append(jnp.where(finals[stretch], state_out, jnp.zeros_like(state_out)))
        state_prev = state_out
    mixed_stream = jnp.concatenate(normed_parts, axis=0)
    endings = lax.all_to_all(
        jnp.stack(ending_parts, axis=0), "seq", split_axis=1, concat_axis=0, tiled=True
    )
    mixed_tokens = lax.all_to_all(mixed_stream, "req", split_axis=0, concat_axis=0, tiled=True)
    normed = gate_and_norm(mixed_tokens, z_in, norm_gain)
    mixed_out = jnp.dot(normed, w_out, preferred_element_type=jnp.float32).astype(jnp.bfloat16)
    return (mixed_out, endings)


def solution(mesh):
    placed = (
        P(("req", "seq"), None),
        P(("req", "seq"), None),
        P(("req", "seq"), None),
        P(("req", "seq"), None),
        P(),
        P(),
        P(),
        P(),
        P(),
        P(),
        P(),
        P(),
    )
    return jax.shard_map(
        per_device,
        mesh=mesh,
        in_specs=placed,
        out_specs=(P(("req", "seq"), None), P("req", "seq", None, None)),
        check_vma=False,
    )
```

```python
import jax
import jax.numpy as jnp
from jax import lax
from jax.sharding import PartitionSpec as P

N = 128
STRETCH = 256


def from_behind(value, axis, steps):
    count = lax.axis_size(axis)
    leading, last = (max(0, -steps), min(count, count - steps))
    return lax.ppermute(value, axis, [(source, source + steps) for source in range(leading, last)])


LMAX_CH = 16


def chain_flat(earlier, later):
    return (earlier[0] * later[0], later[0][:, None] * earlier[1] + later[1])


def carried_in(gain, state, window):
    groups = lax.axis_size("seq")
    heads = gain.shape[0]
    share = heads // groups
    cells = state.shape[1] * state.shape[2]
    packed = jnp.concatenate(
        [state.reshape(heads, cells), jnp.broadcast_to(gain[:, None], (heads, 128))], axis=1
    )
    mine = lax.all_to_all(packed, "seq", split_axis=0, concat_axis=0, tiled=True)
    mine = mine.reshape(groups, share, cells + 128)
    parts = [(mine[k, :, cells], mine[k, :, :cells]) for k in range(groups)]
    prefixes = [(jnp.ones((share,), jnp.float32), jnp.zeros((share, cells), jnp.float32))]
    for k in range(groups):
        prefixes.append(chain_flat(prefixes[-1], parts[k]))
    whole = prefixes[-1]
    reach = -(-window // groups)
    behind = from_behind(whole, "req", reach)
    for step in range(reach - 1, 0, -1):
        behind = chain_flat(behind, from_behind(whole, "req", step))
    incoming = jnp.stack([chain_flat(behind, prefixes[k])[1] for k in range(groups)], axis=0)
    incoming = lax.all_to_all(incoming, "seq", split_axis=0, concat_axis=0, tiled=True)
    return incoming.reshape(state.shape)


def stretch_flags(prompt_stretches, stretch_ids):
    firsts = jnp.cumsum(prompt_stretches) - prompt_stretches
    last_stretches = firsts + prompt_stretches - 1
    starts = jnp.any(stretch_ids[:, None] == firsts[None, :], axis=1)
    finals = jnp.any(stretch_ids[:, None] == last_stretches[None, :], axis=1)
    return (starts, finals)


def causal_conv(row_block, history, weight, conv_bias, starts):
    conv_span = weight.shape[0]
    length = row_block.shape[0]
    extended = jnp.concatenate([history, row_block], axis=0)
    in_stretch = jnp.arange(length, dtype=jnp.int32) % STRETCH
    start_rows = jnp.repeat(starts, STRETCH)
    running = conv_bias[None, :]
    for offset in range(conv_span):
        lag_rows = conv_span - 1 - offset
        shifted = extended[offset : offset + length].astype(jnp.float32)
        usable = jnp.logical_not((in_stretch < lag_rows) & start_rows)
        running = running + weight[offset][None, :] * jnp.where(usable[:, None], shifted, 0.0)
    return jax.nn.silu(running).astype(jnp.bfloat16)


def stretch_summary(x_stretch, bc_stretch, dt_stretch, dt_bias, a_log):
    state_size = bc_stretch.shape[1] // 2
    b_mat = bc_stretch[:, :state_size]
    step_size = jax.nn.softplus(dt_stretch.astype(jnp.float32) + dt_bias[None, :])
    log_decay = jnp.cumsum(-jnp.exp(a_log)[None, :] * step_size, axis=0)
    tail_weight = jnp.exp(log_decay[-1][None, :] - log_decay) * step_size
    weighted_x = (x_stretch.astype(jnp.float32) * tail_weight[:, :, None]).astype(jnp.bfloat16)
    stretch_state = jnp.einsum("uhp,un->hpn", weighted_x, b_mat, preferred_element_type=jnp.float32)
    return (step_size, log_decay, stretch_state)


def stretch_diag(x_stretch, bc_stretch, step_size, log_decay):
    state_size = bc_stretch.shape[1] // 2
    b_mat = bc_stretch[:, :state_size]
    c_mat = bc_stretch[:, state_size:]
    scores = jnp.dot(c_mat, b_mat.T, preferred_element_type=jnp.float32)
    stretch_len = scores.shape[0]
    causal = jnp.arange(stretch_len)[:, None] >= jnp.arange(stretch_len)[None, :]
    by_head = log_decay.T
    segment = by_head[:, :, None] - by_head[:, None, :]
    decay_mask = jnp.where(causal[None], jnp.exp(jnp.where(causal[None], segment, 0.0)), 0.0)
    mixing = (scores[None] * decay_mask * step_size.T[:, None, :]).astype(jnp.bfloat16)
    return jnp.einsum("htu,uhp->thp", mixing, x_stretch, preferred_element_type=jnp.float32)


def finish_stretch(y_diag, log_decay, state_in, x_stretch, c_mat, d_skip):
    state_low = state_in.astype(jnp.bfloat16)
    y_off = jnp.exp(log_decay)[:, :, None] * jnp.einsum(
        "tn,hpn->thp", c_mat, state_low, preferred_element_type=jnp.float32
    )
    mixed_rows = y_diag + y_off + d_skip[None, :, None] * x_stretch.astype(jnp.float32)
    return mixed_rows.reshape(mixed_rows.shape[0], -1).astype(jnp.bfloat16)


def gate_and_norm(mixed_rows, z_rows, norm_gain):
    gated_rows = mixed_rows.astype(jnp.float32) * jax.nn.silu(z_rows.astype(jnp.float32))
    inv_rms = lax.rsqrt(jnp.mean(gated_rows * gated_rows, axis=-1, keepdims=True) + 1e-05)
    return (gated_rows * inv_rms * norm_gain[None, :]).astype(jnp.bfloat16)


def chain_states(earlier, later):
    return (earlier[0] * later[0], later[0][:, None, None] * earlier[1] + later[1])


def per_device(
    x_in,
    bc_in,
    z_in,
    dt_raw,
    conv_weight,
    conv_bias,
    dt_bias,
    a_log,
    d_skip,
    norm_gain,
    w_out,
    prompt_stretches,
):
    n_req = lax.axis_size("req")
    n_seq = lax.axis_size("seq")
    tok_rows, inner_width = x_in.shape
    head_count = a_log.shape[0]
    head_dim = inner_width // head_count
    share = head_count // n_seq
    width = share * head_dim
    chunk = tok_rows // n_req
    bc_width = bc_in.shape[1]
    state_size = bc_width // 2
    conv_span = conv_weight.shape[0]
    group = lax.axis_index("seq")
    block = lax.axis_index("req")

    x_parts = x_in.reshape(n_req, chunk, n_seq, width)
    dt_parts = dt_raw.reshape(n_req, chunk, n_seq, share)
    bc_parts = jnp.broadcast_to(
        bc_in.reshape(n_req, chunk, 1, bc_width), (n_req, chunk, n_seq, bc_width)
    )
    outbound = jnp.concatenate([x_parts, bc_parts, dt_parts], axis=3)
    outbound = outbound.transpose(0, 2, 1, 3).reshape(n_req * n_seq, chunk, -1)
    inbound = lax.all_to_all(outbound, ("req", "seq"), 0, 0, tiled=True)
    inbound = inbound.reshape(n_req, n_seq, chunk, -1).transpose(1, 0, 2, 3)
    inbound = inbound.reshape(n_seq * tok_rows, -1)
    x_rows = inbound[:, :width]
    bc_rows = inbound[:, width : width + bc_width]
    dt_rows = inbound[:, width + bc_width :]

    row_count = x_rows.shape[0]
    stretch_count = row_count // STRETCH
    stretch_ids = block * stretch_count + jnp.arange(stretch_count, dtype=jnp.int32)
    starts, finals = stretch_flags(prompt_stretches, stretch_ids)
    edge_x, edge_bc = from_behind(
        (x_rows[row_count - conv_span + 1 :], bc_rows[row_count - conv_span + 1 :]), "req", 1
    )
    weight_x = lax.dynamic_slice_in_dim(conv_weight, group * width, width, axis=1)
    bias_x = lax.dynamic_slice_in_dim(conv_bias, group * width, width, axis=0)
    conv_x = causal_conv(x_rows, edge_x, weight_x, bias_x, starts)
    conv_bc = causal_conv(
        bc_rows, edge_bc, conv_weight[:, inner_width:], conv_bias[inner_width:], starts
    )
    bias_dt = lax.dynamic_slice_in_dim(dt_bias, group * share, share)
    rate_log = lax.dynamic_slice_in_dim(a_log, group * share, share)
    skip = lax.dynamic_slice_in_dim(d_skip, group * share, share)

    x_heads = conv_x.reshape(stretch_count, STRETCH, share, head_dim)
    bcs = conv_bc.reshape(stretch_count, STRETCH, bc_width)
    b_mat = bcs[:, :, :state_size]
    c_mat = bcs[:, :, state_size:]
    dts = dt_rows.reshape(stretch_count, STRETCH, share)
    step_size = jax.nn.softplus(dts.astype(jnp.float32) + bias_dt[None, None, :])
    log_decay = jnp.cumsum(-jnp.exp(rate_log)[None, None, :] * step_size, axis=1)
    tail_weight = jnp.exp(log_decay[:, -1:, :] - log_decay) * step_size
    weighted_x = (x_heads.astype(jnp.float32) * tail_weight[..., None]).astype(jnp.bfloat16)
    stretch_state = jnp.einsum(
        "cuhp,cun->chpn", weighted_x, b_mat, preferred_element_type=jnp.float32
    )
    carried = jnp.where(starts[:, None], 0.0, jnp.exp(log_decay[:, -1, :]))
    total = (jnp.ones((share,), jnp.float32), jnp.zeros((share, head_dim, N), jnp.float32))
    for stretch in range(stretch_count):
        total = chain_states(total, (carried[stretch], stretch_state[stretch]))
    reach = -(-(LMAX_CH - 1) // stretch_count)
    behind = from_behind(total, "req", reach)
    for step in range(reach - 1, 0, -1):
        behind = chain_states(behind, from_behind(total, "req", step))
    state_prev = behind[1]

    scores = jnp.einsum("ctn,cun->ctu", c_mat, b_mat, preferred_element_type=jnp.float32)
    causal = jnp.arange(STRETCH)[:, None] >= jnp.arange(STRETCH)[None, :]
    by_head = log_decay.transpose(0, 2, 1)
    segment = by_head[:, :, :, None] - by_head[:, :, None, :]
    decay_mask = jnp.where(causal, jnp.exp(jnp.where(causal, segment, 0.0)), 0.0)
    mixing = (
        scores[:, None] * decay_mask * step_size.transpose(0, 2, 1)[:, :, None, :]
    ).astype(jnp.bfloat16)
    y_diag = jnp.einsum("chtu,cuhp->cthp", mixing, x_heads, preferred_element_type=jnp.float32)

    state_ins = []
    ending_parts = []
    for stretch in range(stretch_count):
        state_in = jnp.where(starts[stretch], jnp.zeros_like(state_prev), state_prev)
        state_ins.append(state_in)
        state_out = (
            jnp.exp(log_decay[stretch, -1])[:, None, None] * state_in + stretch_state[stretch]
        )
        ending_parts.append(jnp.where(finals[stretch], state_out, jnp.zeros_like(state_out)))
        state_prev = state_out
    state_low = jnp.stack(state_ins, axis=0).astype(jnp.bfloat16)
    y_off = jnp.exp(log_decay)[..., None] * jnp.einsum(
        "ctn,chpn->cthp", c_mat, state_low, preferred_element_type=jnp.float32
    )
    mixed = y_diag + y_off + skip[None, None, :, None] * x_heads.astype(jnp.float32)
    mixed = mixed.reshape(n_seq, n_req, chunk, width).astype(jnp.bfloat16)
    mixed = mixed.transpose(1, 0, 2, 3).reshape(n_req * n_seq, chunk, width)
    back = lax.all_to_all(mixed, ("req", "seq"), 0, 0, tiled=True)
    back = back.reshape(n_req, n_seq, chunk, width).transpose(0, 2, 1, 3)
    mixed_tokens = back.reshape(tok_rows, inner_width)
    normed = gate_and_norm(mixed_tokens, z_in, norm_gain)
    mixed_out = jnp.dot(normed, w_out, preferred_element_type=jnp.float32).astype(jnp.bfloat16)
    return (mixed_out, jnp.stack(ending_parts, axis=0))


def solution(mesh):
    placed = (
        P(("req", "seq"), None),
        P(("req", "seq"), None),
        P(("req", "seq"), None),
        P(("req", "seq"), None),
        P(),
        P(),
        P(),
        P(),
        P(),
        P(),
        P(),
        P(),
    )
    return jax.shard_map(
        per_device,
        mesh=mesh,
        in_specs=placed,
        out_specs=(P(("req", "seq"), None), P("req", "seq", None, None)),
        check_vma=False,
    )
```

```python
import jax
import jax.numpy as jnp
from jax import lax
from jax.sharding import PartitionSpec as P

N = 128
STRETCH = 256


def from_behind(value, axis, steps):
    count = lax.axis_size(axis)
    leading, last = (max(0, -steps), min(count, count - steps))
    return lax.ppermute(value, axis, [(source, source + steps) for source in range(leading, last)])


LMAX_CH = 16


def chain_flat(earlier, later):
    return (earlier[0] * later[0], later[0][:, None] * earlier[1] + later[1])


def carried_in(gain, state, window):
    groups = lax.axis_size("seq")
    heads = gain.shape[0]
    share = heads // groups
    cells = state.shape[1] * state.shape[2]
    packed = jnp.concatenate(
        [state.reshape(heads, cells), jnp.broadcast_to(gain[:, None], (heads, 128))], axis=1
    )
    mine = lax.all_to_all(packed, "seq", split_axis=0, concat_axis=0, tiled=True)
    mine = mine.reshape(groups, share, cells + 128)
    parts = [(mine[k, :, cells], mine[k, :, :cells]) for k in range(groups)]
    prefixes = [(jnp.ones((share,), jnp.float32), jnp.zeros((share, cells), jnp.float32))]
    for k in range(groups):
        prefixes.append(chain_flat(prefixes[-1], parts[k]))
    whole = prefixes[-1]
    reach = -(-window // groups)
    behind = from_behind(whole, "req", reach)
    for step in range(reach - 1, 0, -1):
        behind = chain_flat(behind, from_behind(whole, "req", step))
    incoming = jnp.stack([chain_flat(behind, prefixes[k])[1] for k in range(groups)], axis=0)
    incoming = lax.all_to_all(incoming, "seq", split_axis=0, concat_axis=0, tiled=True)
    return incoming.reshape(state.shape)


def stretch_flags(prompt_stretches, stretch_ids):
    firsts = jnp.cumsum(prompt_stretches) - prompt_stretches
    last_stretches = firsts + prompt_stretches - 1
    starts = jnp.any(stretch_ids[:, None] == firsts[None, :], axis=1)
    finals = jnp.any(stretch_ids[:, None] == last_stretches[None, :], axis=1)
    return (starts, finals)


def causal_conv(row_block, history, weight, conv_bias, starts):
    conv_span = weight.shape[0]
    length = row_block.shape[0]
    extended = jnp.concatenate([history, row_block], axis=0)
    in_stretch = jnp.arange(length, dtype=jnp.int32) % STRETCH
    start_rows = jnp.repeat(starts, STRETCH)
    running = conv_bias[None, :]
    for offset in range(conv_span):
        lag_rows = conv_span - 1 - offset
        shifted = extended[offset : offset + length].astype(jnp.float32)
        usable = jnp.logical_not((in_stretch < lag_rows) & start_rows)
        running = running + weight[offset][None, :] * jnp.where(usable[:, None], shifted, 0.0)
    return jax.nn.silu(running).astype(jnp.bfloat16)


def stretch_summary(x_stretch, bc_stretch, dt_stretch, dt_bias, a_log):
    state_size = bc_stretch.shape[1] // 2
    b_mat = bc_stretch[:, :state_size]
    step_size = jax.nn.softplus(dt_stretch.astype(jnp.float32) + dt_bias[None, :])
    log_decay = jnp.cumsum(-jnp.exp(a_log)[None, :] * step_size, axis=0)
    tail_weight = jnp.exp(log_decay[-1][None, :] - log_decay) * step_size
    weighted_x = (x_stretch.astype(jnp.float32) * tail_weight[:, :, None]).astype(jnp.bfloat16)
    stretch_state = jnp.einsum("uhp,un->hpn", weighted_x, b_mat, preferred_element_type=jnp.float32)
    return (step_size, log_decay, stretch_state)


def stretch_diag(x_stretch, bc_stretch, step_size, log_decay):
    state_size = bc_stretch.shape[1] // 2
    b_mat = bc_stretch[:, :state_size]
    c_mat = bc_stretch[:, state_size:]
    scores = jnp.dot(c_mat, b_mat.T, preferred_element_type=jnp.float32)
    stretch_len = scores.shape[0]
    causal = jnp.arange(stretch_len)[:, None] >= jnp.arange(stretch_len)[None, :]
    by_head = log_decay.T
    segment = by_head[:, :, None] - by_head[:, None, :]
    decay_mask = jnp.where(causal[None], jnp.exp(jnp.where(causal[None], segment, 0.0)), 0.0)
    mixing = (scores[None] * decay_mask * step_size.T[:, None, :]).astype(jnp.bfloat16)
    return jnp.einsum("htu,uhp->thp", mixing, x_stretch, preferred_element_type=jnp.float32)


def finish_stretch(y_diag, log_decay, state_in, x_stretch, c_mat, d_skip):
    state_low = state_in.astype(jnp.bfloat16)
    y_off = jnp.exp(log_decay)[:, :, None] * jnp.einsum(
        "tn,hpn->thp", c_mat, state_low, preferred_element_type=jnp.float32
    )
    mixed_rows = y_diag + y_off + d_skip[None, :, None] * x_stretch.astype(jnp.float32)
    return mixed_rows.reshape(mixed_rows.shape[0], -1).astype(jnp.bfloat16)


def gate_and_norm(mixed_rows, z_rows, norm_gain):
    gated_rows = mixed_rows.astype(jnp.float32) * jax.nn.silu(z_rows.astype(jnp.float32))
    inv_rms = lax.rsqrt(jnp.mean(gated_rows * gated_rows, axis=-1, keepdims=True) + 1e-05)
    return (gated_rows * inv_rms * norm_gain[None, :]).astype(jnp.bfloat16)


def chain_states(earlier, later):
    return (earlier[0] * later[0], later[0][:, None, None] * earlier[1] + later[1])


def per_device(
    x_in,
    bc_in,
    z_in,
    dt_raw,
    conv_weight,
    conv_bias,
    dt_bias,
    a_log,
    d_skip,
    norm_gain,
    w_out,
    prompt_stretches,
):
    n_req = lax.axis_size("req")
    n_seq = lax.axis_size("seq")
    tok_rows, inner_width = x_in.shape
    head_count = a_log.shape[0]
    head_dim = inner_width // head_count
    share = head_count // n_seq
    width = share * head_dim
    chunk = tok_rows // n_req
    bc_width = bc_in.shape[1]
    state_size = bc_width // 2
    conv_span = conv_weight.shape[0]
    group = lax.axis_index("seq")
    block = lax.axis_index("req")

    x_slabs = jnp.stack([x_in[:, g * width : (g + 1) * width] for g in range(n_seq)], axis=0)
    dt_slabs = jnp.stack([dt_raw[:, g * share : (g + 1) * share] for g in range(n_seq)], axis=0)
    bc_slabs = jnp.broadcast_to(bc_in[None], (n_seq, tok_rows, bc_width))
    outbound = jnp.concatenate([x_slabs, bc_slabs, dt_slabs], axis=2)
    outbound = outbound.reshape(n_seq * n_req, chunk, -1)
    inbound = lax.all_to_all(outbound, ("seq", "req"), 0, 0, tiled=True)
    inbound = inbound.reshape(n_seq * tok_rows, -1)
    x_rows = inbound[:, :width]
    bc_rows = inbound[:, width : width + bc_width]
    dt_rows = inbound[:, width + bc_width :]

    row_count = x_rows.shape[0]
    stretch_count = row_count // STRETCH
    stretch_ids = block * stretch_count + jnp.arange(stretch_count, dtype=jnp.int32)
    starts, finals = stretch_flags(prompt_stretches, stretch_ids)
    edge_x, edge_bc = from_behind(
        (x_rows[row_count - conv_span + 1 :], bc_rows[row_count - conv_span + 1 :]), "req", 1
    )
    weight_x = lax.dynamic_slice_in_dim(conv_weight, group * width, width, axis=1)
    bias_x = lax.dynamic_slice_in_dim(conv_bias, group * width, width, axis=0)
    conv_x = causal_conv(x_rows, edge_x, weight_x, bias_x, starts)
    conv_bc = causal_conv(
        bc_rows, edge_bc, conv_weight[:, inner_width:], conv_bias[inner_width:], starts
    )
    bias_dt = lax.dynamic_slice_in_dim(dt_bias, group * share, share)
    rate_log = lax.dynamic_slice_in_dim(a_log, group * share, share)
    skip = lax.dynamic_slice_in_dim(d_skip, group * share, share)

    x_heads = conv_x.reshape(stretch_count, STRETCH, share, head_dim)
    bcs = conv_bc.reshape(stretch_count, STRETCH, bc_width)
    b_mat = bcs[:, :, :state_size]
    c_mat = bcs[:, :, state_size:]
    dts = dt_rows.reshape(stretch_count, STRETCH, share)
    step_size = jax.nn.softplus(dts.astype(jnp.float32) + bias_dt[None, None, :])
    log_decay = jnp.cumsum(-jnp.exp(rate_log)[None, None, :] * step_size, axis=1)
    tail_weight = jnp.exp(log_decay[:, -1:, :] - log_decay) * step_size
    weighted_x = (x_heads.astype(jnp.float32) * tail_weight[..., None]).astype(jnp.bfloat16)
    stretch_state = jnp.einsum(
        "cuhp,cun->chpn", weighted_x, b_mat, preferred_element_type=jnp.float32
    )
    carried = jnp.where(starts[:, None], 0.0, jnp.exp(log_decay[:, -1, :]))
    total = (jnp.ones((share,), jnp.float32), jnp.zeros((share, head_dim, N), jnp.float32))
    for stretch in range(stretch_count):
        total = chain_states(total, (carried[stretch], stretch_state[stretch]))
    reach = -(-(LMAX_CH - 1) // stretch_count)
    behind = from_behind(total, "req", reach)
    for step in range(reach - 1, 0, -1):
        behind = chain_states(behind, from_behind(total, "req", step))
    state_prev = behind[1]

    scores = jnp.einsum("ctn,cun->ctu", c_mat, b_mat, preferred_element_type=jnp.float32)
    causal = jnp.arange(STRETCH)[:, None] >= jnp.arange(STRETCH)[None, :]
    by_head = log_decay.transpose(0, 2, 1)
    segment = by_head[:, :, :, None] - by_head[:, :, None, :]
    decay_mask = jnp.where(causal, jnp.exp(jnp.where(causal, segment, 0.0)), 0.0)
    mixing = (
        scores[:, None] * decay_mask * step_size.transpose(0, 2, 1)[:, :, None, :]
    ).astype(jnp.bfloat16)
    y_diag = jnp.einsum("chtu,cuhp->cthp", mixing, x_heads, preferred_element_type=jnp.float32)

    state_ins = []
    ending_parts = []
    for stretch in range(stretch_count):
        state_in = jnp.where(starts[stretch], jnp.zeros_like(state_prev), state_prev)
        state_ins.append(state_in)
        state_out = (
            jnp.exp(log_decay[stretch, -1])[:, None, None] * state_in + stretch_state[stretch]
        )
        ending_parts.append(jnp.where(finals[stretch], state_out, jnp.zeros_like(state_out)))
        state_prev = state_out
    state_low = jnp.stack(state_ins, axis=0).astype(jnp.bfloat16)
    state_low = state_low.reshape(stretch_count, width, N)
    y_off = jnp.repeat(jnp.exp(log_decay), head_dim, axis=-1) * jnp.einsum(
        "ctn,cqn->ctq", c_mat, state_low, preferred_element_type=jnp.float32
    )
    y_diag = jnp.concatenate(
        [
            jnp.einsum(
                "ctu,cup->ctp", mixing[:, h], x_heads[:, :, h], preferred_element_type=jnp.float32
            )
            for h in range(share)
        ],
        axis=-1,
    )
    x_flat = conv_x.reshape(stretch_count, STRETCH, width).astype(jnp.float32)
    mixed = y_diag + y_off + jnp.repeat(skip, head_dim)[None, None, :] * x_flat
    mixed = mixed.astype(jnp.bfloat16).reshape(n_seq * n_req, chunk, width)
    back = lax.all_to_all(mixed, ("seq", "req"), 0, 0, tiled=True)
    back = back.reshape(n_seq, tok_rows, width)
    mixed_tokens = jnp.concatenate([back[g] for g in range(n_seq)], axis=1)
    normed = gate_and_norm(mixed_tokens, z_in, norm_gain)
    mixed_out = jnp.dot(normed, w_out, preferred_element_type=jnp.float32).astype(jnp.bfloat16)
    return (mixed_out, jnp.stack(ending_parts, axis=0))


def solution(mesh):
    placed = (
        P(("req", "seq"), None),
        P(("req", "seq"), None),
        P(("req", "seq"), None),
        P(("req", "seq"), None),
        P(),
        P(),
        P(),
        P(),
        P(),
        P(),
        P(),
        P(),
    )
    return jax.shard_map(
        per_device,
        mesh=mesh,
        in_specs=placed,
        out_specs=(P(("req", "seq"), None), P("req", "seq", None, None)),
        check_vma=False,
    )
```

```python
import jax
import jax.numpy as jnp
from jax import lax
from jax.sharding import PartitionSpec as P

N = 128
STRETCH = 256


def from_behind(value, axis, steps):
    count = lax.axis_size(axis)
    leading, last = (max(0, -steps), min(count, count - steps))
    return lax.ppermute(value, axis, [(source, source + steps) for source in range(leading, last)])


LMAX_CH = 16


def chain_flat(earlier, later):
    return (earlier[0] * later[0], later[0][:, None] * earlier[1] + later[1])


def carried_in(gain, state, window):
    groups = lax.axis_size("seq")
    heads = gain.shape[0]
    share = heads // groups
    cells = state.shape[1] * state.shape[2]
    packed = jnp.concatenate(
        [state.reshape(heads, cells), jnp.broadcast_to(gain[:, None], (heads, 128))], axis=1
    )
    mine = lax.all_to_all(packed, "seq", split_axis=0, concat_axis=0, tiled=True)
    mine = mine.reshape(groups, share, cells + 128)
    parts = [(mine[k, :, cells], mine[k, :, :cells]) for k in range(groups)]
    prefixes = [(jnp.ones((share,), jnp.float32), jnp.zeros((share, cells), jnp.float32))]
    for k in range(groups):
        prefixes.append(chain_flat(prefixes[-1], parts[k]))
    whole = prefixes[-1]
    reach = -(-window // groups)
    behind = from_behind(whole, "req", reach)
    for step in range(reach - 1, 0, -1):
        behind = chain_flat(behind, from_behind(whole, "req", step))
    incoming = jnp.stack([chain_flat(behind, prefixes[k])[1] for k in range(groups)], axis=0)
    incoming = lax.all_to_all(incoming, "seq", split_axis=0, concat_axis=0, tiled=True)
    return incoming.reshape(state.shape)


def stretch_flags(prompt_stretches, stretch_ids):
    firsts = jnp.cumsum(prompt_stretches) - prompt_stretches
    last_stretches = firsts + prompt_stretches - 1
    starts = jnp.any(stretch_ids[:, None] == firsts[None, :], axis=1)
    finals = jnp.any(stretch_ids[:, None] == last_stretches[None, :], axis=1)
    return (starts, finals)


def causal_conv(row_block, history, weight, conv_bias, starts):
    conv_span = weight.shape[0]
    length = row_block.shape[0]
    extended = jnp.concatenate([history, row_block], axis=0)
    in_stretch = jnp.arange(length, dtype=jnp.int32) % STRETCH
    start_rows = jnp.repeat(starts, STRETCH)
    running = conv_bias[None, :]
    for offset in range(conv_span):
        lag_rows = conv_span - 1 - offset
        shifted = extended[offset : offset + length].astype(jnp.float32)
        usable = jnp.logical_not((in_stretch < lag_rows) & start_rows)
        running = running + weight[offset][None, :] * jnp.where(usable[:, None], shifted, 0.0)
    return jax.nn.silu(running).astype(jnp.bfloat16)


def stretch_summary(x_stretch, bc_stretch, dt_stretch, dt_bias, a_log):
    state_size = bc_stretch.shape[1] // 2
    b_mat = bc_stretch[:, :state_size]
    step_size = jax.nn.softplus(dt_stretch.astype(jnp.float32) + dt_bias[None, :])
    log_decay = jnp.cumsum(-jnp.exp(a_log)[None, :] * step_size, axis=0)
    tail_weight = jnp.exp(log_decay[-1][None, :] - log_decay) * step_size
    weighted_x = (x_stretch.astype(jnp.float32) * tail_weight[:, :, None]).astype(jnp.bfloat16)
    stretch_state = jnp.einsum("uhp,un->hpn", weighted_x, b_mat, preferred_element_type=jnp.float32)
    return (step_size, log_decay, stretch_state)


def stretch_diag(x_stretch, bc_stretch, step_size, log_decay):
    state_size = bc_stretch.shape[1] // 2
    b_mat = bc_stretch[:, :state_size]
    c_mat = bc_stretch[:, state_size:]
    scores = jnp.dot(c_mat, b_mat.T, preferred_element_type=jnp.float32)
    stretch_len = scores.shape[0]
    causal = jnp.arange(stretch_len)[:, None] >= jnp.arange(stretch_len)[None, :]
    by_head = log_decay.T
    segment = by_head[:, :, None] - by_head[:, None, :]
    decay_mask = jnp.where(causal[None], jnp.exp(jnp.where(causal[None], segment, 0.0)), 0.0)
    mixing = (scores[None] * decay_mask * step_size.T[:, None, :]).astype(jnp.bfloat16)
    return jnp.einsum("htu,uhp->thp", mixing, x_stretch, preferred_element_type=jnp.float32)


def finish_stretch(y_diag, log_decay, state_in, x_stretch, c_mat, d_skip):
    state_low = state_in.astype(jnp.bfloat16)
    y_off = jnp.exp(log_decay)[:, :, None] * jnp.einsum(
        "tn,hpn->thp", c_mat, state_low, preferred_element_type=jnp.float32
    )
    mixed_rows = y_diag + y_off + d_skip[None, :, None] * x_stretch.astype(jnp.float32)
    return mixed_rows.reshape(mixed_rows.shape[0], -1).astype(jnp.bfloat16)


def gate_and_norm(mixed_rows, z_rows, norm_gain):
    gated_rows = mixed_rows.astype(jnp.float32) * jax.nn.silu(z_rows.astype(jnp.float32))
    inv_rms = lax.rsqrt(jnp.mean(gated_rows * gated_rows, axis=-1, keepdims=True) + 1e-05)
    return (gated_rows * inv_rms * norm_gain[None, :]).astype(jnp.bfloat16)


def chain_states(earlier, later):
    return (earlier[0] * later[0], later[0][:, None, None] * earlier[1] + later[1])


def per_device(
    x_in,
    bc_in,
    z_in,
    dt_raw,
    conv_weight,
    conv_bias,
    dt_bias,
    a_log,
    d_skip,
    norm_gain,
    w_out,
    prompt_stretches,
):
    n_req = lax.axis_size("req")
    n_seq = lax.axis_size("seq")
    tok_rows, inner_width = x_in.shape
    head_count = a_log.shape[0]
    head_dim = inner_width // head_count
    share = head_count // n_seq
    width = share * head_dim
    chunk = tok_rows // n_req
    bc_width = bc_in.shape[1]
    state_size = bc_width // 2
    conv_span = conv_weight.shape[0]
    group = lax.axis_index("seq")
    block = lax.axis_index("req")

    x_slabs = jnp.stack([x_in[:, g * width : (g + 1) * width] for g in range(n_seq)], axis=0)
    dt_slabs = jnp.stack([dt_raw[:, g * share : (g + 1) * share] for g in range(n_seq)], axis=0)
    bc_slabs = jnp.broadcast_to(bc_in[None], (n_seq, tok_rows, bc_width))
    outbound = jnp.concatenate([x_slabs, bc_slabs, dt_slabs], axis=2)
    outbound = outbound.reshape(n_seq * n_req, chunk, -1)
    inbound = lax.all_to_all(outbound, ("seq", "req"), 0, 0, tiled=True)
    inbound = inbound.reshape(n_seq * tok_rows, -1)
    x_rows = inbound[:, :width]
    bc_rows = inbound[:, width : width + bc_width]
    dt_rows = inbound[:, width + bc_width :]

    row_count = x_rows.shape[0]
    stretch_count = row_count // STRETCH
    stretch_ids = block * stretch_count + jnp.arange(stretch_count, dtype=jnp.int32)
    starts, finals = stretch_flags(prompt_stretches, stretch_ids)
    edge_x, edge_bc = from_behind(
        (x_rows[row_count - conv_span + 1 :], bc_rows[row_count - conv_span + 1 :]), "req", 1
    )
    weight_x = lax.dynamic_slice_in_dim(conv_weight, group * width, width, axis=1)
    bias_x = lax.dynamic_slice_in_dim(conv_bias, group * width, width, axis=0)
    conv_x = causal_conv(x_rows, edge_x, weight_x, bias_x, starts)
    conv_bc = causal_conv(
        bc_rows, edge_bc, conv_weight[:, inner_width:], conv_bias[inner_width:], starts
    )
    bias_dt = lax.dynamic_slice_in_dim(dt_bias, group * share, share)
    rate_log = lax.dynamic_slice_in_dim(a_log, group * share, share)
    skip = lax.dynamic_slice_in_dim(d_skip, group * share, share)

    x_heads = conv_x.reshape(stretch_count, STRETCH, share, head_dim)
    bcs = conv_bc.reshape(stretch_count, STRETCH, bc_width)
    b_mat = bcs[:, :, :state_size]
    c_mat = bcs[:, :, state_size:]
    dts = dt_rows.reshape(stretch_count, STRETCH, share)
    step_size = jax.nn.softplus(dts.astype(jnp.float32) + bias_dt[None, None, :])
    log_decay = jnp.cumsum(-jnp.exp(rate_log)[None, None, :] * step_size, axis=1)
    tail_weight = jnp.exp(log_decay[:, -1:, :] - log_decay) * step_size
    weighted_x = (x_heads.astype(jnp.float32) * tail_weight[..., None]).astype(jnp.bfloat16)
    stretch_state = jnp.einsum(
        "cuhp,cun->chpn", weighted_x, b_mat, preferred_element_type=jnp.float32
    )
    carried = jnp.where(starts[:, None], 0.0, jnp.exp(log_decay[:, -1, :]))
    total = (jnp.ones((share,), jnp.float32), jnp.zeros((share, head_dim, N), jnp.float32))
    for stretch in range(stretch_count):
        total = chain_states(total, (carried[stretch], stretch_state[stretch]))
    reach = -(-(LMAX_CH - 1) // stretch_count)
    behind = from_behind(total, "req", reach)
    for step in range(reach - 1, 0, -1):
        behind = chain_states(behind, from_behind(total, "req", step))
    state_prev = behind[1]

    scores = jnp.einsum("ctn,cun->ctu", c_mat, b_mat, preferred_element_type=jnp.float32)
    causal = jnp.arange(STRETCH)[:, None] >= jnp.arange(STRETCH)[None, :]
    by_head = log_decay.transpose(0, 2, 1)
    segment = by_head[:, :, :, None] - by_head[:, :, None, :]
    decay_mask = jnp.where(causal, jnp.exp(jnp.where(causal, segment, 0.0)), 0.0)
    mixing = (
        scores[:, None] * decay_mask * step_size.transpose(0, 2, 1)[:, :, None, :]
    ).astype(jnp.bfloat16)
    y_diag = jnp.einsum("chtu,cuhp->cthp", mixing, x_heads, preferred_element_type=jnp.float32)

    keep = jnp.where(starts, 0.0, 1.0)
    gains = jnp.exp(log_decay[:, -1, :])
    rows = []
    weights = [jnp.zeros((share,), jnp.float32)] * stretch_count + [jnp.ones((share,), jnp.float32)]
    for stretch in range(stretch_count):
        if stretch > 0:
            weights = [w * gains[stretch - 1] for w in weights]
            weights[stretch - 1] = weights[stretch - 1] + 1.0
        weights = [w * keep[stretch] for w in weights]
        rows.append(jnp.stack(weights, axis=0))
    mix = jnp.stack(rows, axis=0)
    sources = jnp.concatenate([stretch_state, state_prev[None]], axis=0)
    state_in_all = jnp.einsum(
        "ckh,khpn->chpn", mix, sources, precision=lax.Precision.HIGHEST,
        preferred_element_type=jnp.float32,
    )
    state_out_all = gains[:, :, None, None] * state_in_all + stretch_state
    endings = jnp.where(finals[:, None, None, None], state_out_all, 0.0)
    state_ins = [state_in_all[c] for c in range(stretch_count)]
    state_low = jnp.stack(state_ins, axis=0).astype(jnp.bfloat16)
    state_low = state_low.reshape(stretch_count, width, N)
    y_off = jnp.repeat(jnp.exp(log_decay), head_dim, axis=-1) * jnp.einsum(
        "ctn,cqn->ctq", c_mat, state_low, preferred_element_type=jnp.float32
    )
    y_diag = jnp.concatenate(
        [
            jnp.einsum(
                "ctu,cup->ctp", mixing[:, h], x_heads[:, :, h], preferred_element_type=jnp.float32
            )
            for h in range(share)
        ],
        axis=-1,
    )
    x_flat = conv_x.reshape(stretch_count, STRETCH, width).astype(jnp.float32)
    mixed = y_diag + y_off + jnp.repeat(skip, head_dim)[None, None, :] * x_flat
    mixed = mixed.astype(jnp.bfloat16).reshape(n_seq * n_req, chunk, width)
    back = lax.all_to_all(mixed, ("seq", "req"), 0, 0, tiled=True)
    back = back.reshape(n_seq, tok_rows, width)
    mixed_tokens = jnp.concatenate([back[g] for g in range(n_seq)], axis=1)
    normed = gate_and_norm(mixed_tokens, z_in, norm_gain)
    mixed_out = jnp.dot(normed, w_out, preferred_element_type=jnp.float32).astype(jnp.bfloat16)
    return (mixed_out, endings)


def solution(mesh):
    placed = (
        P(("req", "seq"), None),
        P(("req", "seq"), None),
        P(("req", "seq"), None),
        P(("req", "seq"), None),
        P(),
        P(),
        P(),
        P(),
        P(),
        P(),
        P(),
        P(),
    )
    return jax.shard_map(
        per_device,
        mesh=mesh,
        in_specs=placed,
        out_specs=(P(("req", "seq"), None), P("req", "seq", None, None)),
        check_vma=False,
    )
```

```python
import jax
import jax.numpy as jnp
from jax import lax
from jax.sharding import PartitionSpec as P

N = 128
STRETCH = 256


def from_behind(value, axis, steps):
    count = lax.axis_size(axis)
    leading, last = (max(0, -steps), min(count, count - steps))
    return lax.ppermute(value, axis, [(source, source + steps) for source in range(leading, last)])


LMAX_CH = 16


def chain_flat(earlier, later):
    return (earlier[0] * later[0], later[0][:, None] * earlier[1] + later[1])


def carried_in(gain, state, window):
    groups = lax.axis_size("seq")
    heads = gain.shape[0]
    share = heads // groups
    cells = state.shape[1] * state.shape[2]
    packed = jnp.concatenate(
        [state.reshape(heads, cells), jnp.broadcast_to(gain[:, None], (heads, 128))], axis=1
    )
    mine = lax.all_to_all(packed, "seq", split_axis=0, concat_axis=0, tiled=True)
    mine = mine.reshape(groups, share, cells + 128)
    parts = [(mine[k, :, cells], mine[k, :, :cells]) for k in range(groups)]
    prefixes = [(jnp.ones((share,), jnp.float32), jnp.zeros((share, cells), jnp.float32))]
    for k in range(groups):
        prefixes.append(chain_flat(prefixes[-1], parts[k]))
    whole = prefixes[-1]
    reach = -(-window // groups)
    behind = from_behind(whole, "req", reach)
    for step in range(reach - 1, 0, -1):
        behind = chain_flat(behind, from_behind(whole, "req", step))
    incoming = jnp.stack([chain_flat(behind, prefixes[k])[1] for k in range(groups)], axis=0)
    incoming = lax.all_to_all(incoming, "seq", split_axis=0, concat_axis=0, tiled=True)
    return incoming.reshape(state.shape)


def stretch_flags(prompt_stretches, stretch_ids):
    firsts = jnp.cumsum(prompt_stretches) - prompt_stretches
    last_stretches = firsts + prompt_stretches - 1
    starts = jnp.any(stretch_ids[:, None] == firsts[None, :], axis=1)
    finals = jnp.any(stretch_ids[:, None] == last_stretches[None, :], axis=1)
    return (starts, finals)


def causal_conv(row_block, history, weight, conv_bias, starts):
    conv_span = weight.shape[0]
    length = row_block.shape[0]
    extended = jnp.concatenate([history, row_block], axis=0)
    in_stretch = jnp.arange(length, dtype=jnp.int32) % STRETCH
    start_rows = jnp.repeat(starts, STRETCH)
    running = conv_bias[None, :]
    for offset in range(conv_span):
        lag_rows = conv_span - 1 - offset
        shifted = extended[offset : offset + length].astype(jnp.float32)
        usable = jnp.logical_not((in_stretch < lag_rows) & start_rows)
        running = running + weight[offset][None, :] * jnp.where(usable[:, None], shifted, 0.0)
    return jax.nn.silu(running).astype(jnp.bfloat16)


def stretch_summary(x_stretch, bc_stretch, dt_stretch, dt_bias, a_log):
    state_size = bc_stretch.shape[1] // 2
    b_mat = bc_stretch[:, :state_size]
    step_size = jax.nn.softplus(dt_stretch.astype(jnp.float32) + dt_bias[None, :])
    log_decay = jnp.cumsum(-jnp.exp(a_log)[None, :] * step_size, axis=0)
    tail_weight = jnp.exp(log_decay[-1][None, :] - log_decay) * step_size
    weighted_x = (x_stretch.astype(jnp.float32) * tail_weight[:, :, None]).astype(jnp.bfloat16)
    stretch_state = jnp.einsum("uhp,un->hpn", weighted_x, b_mat, preferred_element_type=jnp.float32)
    return (step_size, log_decay, stretch_state)


def stretch_diag(x_stretch, bc_stretch, step_size, log_decay):
    state_size = bc_stretch.shape[1] // 2
    b_mat = bc_stretch[:, :state_size]
    c_mat = bc_stretch[:, state_size:]
    scores = jnp.dot(c_mat, b_mat.T, preferred_element_type=jnp.float32)
    stretch_len = scores.shape[0]
    causal = jnp.arange(stretch_len)[:, None] >= jnp.arange(stretch_len)[None, :]
    by_head = log_decay.T
    segment = by_head[:, :, None] - by_head[:, None, :]
    decay_mask = jnp.where(causal[None], jnp.exp(jnp.where(causal[None], segment, 0.0)), 0.0)
    mixing = (scores[None] * decay_mask * step_size.T[:, None, :]).astype(jnp.bfloat16)
    return jnp.einsum("htu,uhp->thp", mixing, x_stretch, preferred_element_type=jnp.float32)


def finish_stretch(y_diag, log_decay, state_in, x_stretch, c_mat, d_skip):
    state_low = state_in.astype(jnp.bfloat16)
    y_off = jnp.exp(log_decay)[:, :, None] * jnp.einsum(
        "tn,hpn->thp", c_mat, state_low, preferred_element_type=jnp.float32
    )
    mixed_rows = y_diag + y_off + d_skip[None, :, None] * x_stretch.astype(jnp.float32)
    return mixed_rows.reshape(mixed_rows.shape[0], -1).astype(jnp.bfloat16)


def gate_and_norm(mixed_rows, z_rows, norm_gain):
    gated_rows = mixed_rows.astype(jnp.float32) * jax.nn.silu(z_rows.astype(jnp.float32))
    inv_rms = lax.rsqrt(jnp.mean(gated_rows * gated_rows, axis=-1, keepdims=True) + 1e-05)
    return (gated_rows * inv_rms * norm_gain[None, :]).astype(jnp.bfloat16)


def chain_states(earlier, later):
    return (earlier[0] * later[0], later[0][:, None, None] * earlier[1] + later[1])


def per_device(
    x_in,
    bc_in,
    z_in,
    dt_raw,
    conv_weight,
    conv_bias,
    dt_bias,
    a_log,
    d_skip,
    norm_gain,
    w_out,
    prompt_stretches,
):
    n_req = lax.axis_size("req")
    n_seq = lax.axis_size("seq")
    tok_rows, inner_width = x_in.shape
    head_count = a_log.shape[0]
    head_dim = inner_width // head_count
    share = head_count // n_seq
    width = share * head_dim
    chunk = tok_rows // n_req
    bc_width = bc_in.shape[1]
    state_size = bc_width // 2
    conv_span = conv_weight.shape[0]
    group = lax.axis_index("seq")
    block = lax.axis_index("req")

    x_slabs = jnp.stack([x_in[:, g * width : (g + 1) * width] for g in range(n_seq)], axis=0)
    dt_slabs = jnp.stack([dt_raw[:, g * share : (g + 1) * share] for g in range(n_seq)], axis=0)
    bc_slabs = jnp.broadcast_to(bc_in[None], (n_seq, tok_rows, bc_width))
    outbound = jnp.concatenate([x_slabs, bc_slabs, dt_slabs], axis=2)
    outbound = outbound.reshape(n_seq * n_req, chunk, -1)
    inbound = lax.all_to_all(outbound, ("seq", "req"), 0, 0, tiled=True)
    inbound = inbound.reshape(n_seq * tok_rows, -1)
    x_rows = inbound[:, :width]
    bc_rows = inbound[:, width : width + bc_width]
    dt_rows = inbound[:, width + bc_width :]

    row_count = x_rows.shape[0]
    stretch_count = row_count // STRETCH
    stretch_ids = block * stretch_count + jnp.arange(stretch_count, dtype=jnp.int32)
    starts, finals = stretch_flags(prompt_stretches, stretch_ids)
    edge_x, edge_bc = from_behind(
        (x_rows[row_count - conv_span + 1 :], bc_rows[row_count - conv_span + 1 :]), "req", 1
    )
    weight_x = lax.dynamic_slice_in_dim(conv_weight, group * width, width, axis=1)
    bias_x = lax.dynamic_slice_in_dim(conv_bias, group * width, width, axis=0)
    conv_x = causal_conv(x_rows, edge_x, weight_x, bias_x, starts)
    conv_bc = causal_conv(
        bc_rows, edge_bc, conv_weight[:, inner_width:], conv_bias[inner_width:], starts
    )
    bias_dt = lax.dynamic_slice_in_dim(dt_bias, group * share, share)
    rate_log = lax.dynamic_slice_in_dim(a_log, group * share, share)
    skip = lax.dynamic_slice_in_dim(d_skip, group * share, share)

    x_heads = conv_x.reshape(stretch_count, STRETCH, share, head_dim)
    bcs = conv_bc.reshape(stretch_count, STRETCH, bc_width)
    b_mat = bcs[:, :, :state_size]
    c_mat = bcs[:, :, state_size:]
    dts = dt_rows.reshape(stretch_count, STRETCH, share)
    step_size = jax.nn.softplus(dts.astype(jnp.float32) + bias_dt[None, None, :])
    log_decay = jnp.cumsum(-jnp.exp(rate_log)[None, None, :] * step_size, axis=1)
    tail_weight = jnp.exp(log_decay[:, -1:, :] - log_decay) * step_size
    weighted_x = (x_heads.astype(jnp.float32) * tail_weight[..., None]).astype(jnp.bfloat16)
    stretch_state = jnp.einsum(
        "cuhp,cun->chpn", weighted_x, b_mat, preferred_element_type=jnp.float32
    )
    carried = jnp.where(starts[:, None], 0.0, jnp.exp(log_decay[:, -1, :]))
    total = (jnp.ones((share,), jnp.float32), jnp.zeros((share, head_dim, N), jnp.float32))
    for stretch in range(stretch_count):
        total = chain_states(total, (carried[stretch], stretch_state[stretch]))
    reach = -(-(LMAX_CH - 1) // stretch_count)
    behind = from_behind(total, "req", reach)
    for step in range(reach - 1, 0, -1):
        behind = chain_states(behind, from_behind(total, "req", step))
    state_prev = behind[1]

    scores = jnp.einsum("ctn,cun->ctu", c_mat, b_mat, preferred_element_type=jnp.float32)
    causal = jnp.arange(STRETCH)[:, None] >= jnp.arange(STRETCH)[None, :]
    by_head = log_decay.transpose(0, 2, 1)
    segment = by_head[:, :, :, None] - by_head[:, :, None, :]
    decay_mask = jnp.where(causal, jnp.exp(jnp.where(causal, segment, 0.0)), 0.0)
    mixing = (
        scores[:, None] * decay_mask * step_size.transpose(0, 2, 1)[:, :, None, :]
    ).astype(jnp.bfloat16)
    y_diag = jnp.einsum("chtu,cuhp->cthp", mixing, x_heads, preferred_element_type=jnp.float32)

    state_ins = []
    ending_parts = []
    for stretch in range(stretch_count):
        state_in = jnp.where(starts[stretch], jnp.zeros_like(state_prev), state_prev)
        state_ins.append(state_in)
        state_out = (
            jnp.exp(log_decay[stretch, -1])[:, None, None] * state_in + stretch_state[stretch]
        )
        ending_parts.append(jnp.where(finals[stretch], state_out, jnp.zeros_like(state_out)))
        state_prev = state_out
    state_low = jnp.stack(state_ins, axis=0).astype(jnp.bfloat16)
    state_low = state_low.reshape(stretch_count, width, N)
    split = 4 if share > 4 else share
    pieces = []
    for lo, hi in ((0, split), (split, share)):
        if lo == hi:
            continue
        cols = slice(lo * head_dim, hi * head_dim)
        y_off = jnp.repeat(jnp.exp(log_decay[:, :, lo:hi]), head_dim, axis=-1) * jnp.einsum(
            "ctn,cqn->ctq", c_mat, state_low[:, cols], preferred_element_type=jnp.float32
        )
        y_diag = jnp.concatenate(
            [
                jnp.einsum(
                    "ctu,cup->ctp", mixing[:, h], x_heads[:, :, h],
                    preferred_element_type=jnp.float32,
                )
                for h in range(lo, hi)
            ],
            axis=-1,
        )
        x_flat = conv_x.reshape(stretch_count, STRETCH, width)[:, :, cols].astype(jnp.float32)
        mixed = y_diag + y_off + jnp.repeat(skip[lo:hi], head_dim)[None, None, :] * x_flat
        mixed = mixed.astype(jnp.bfloat16).reshape(n_seq * n_req, chunk, (hi - lo) * head_dim)
        back = lax.all_to_all(mixed, ("seq", "req"), 0, 0, tiled=True)
        pieces.append(back.reshape(n_seq, tok_rows, (hi - lo) * head_dim))
    mixed_tokens = jnp.concatenate(
        [piece[g] for g in range(n_seq) for piece in pieces], axis=1
    )
    normed = gate_and_norm(mixed_tokens, z_in, norm_gain)
    mixed_out = jnp.dot(normed, w_out, preferred_element_type=jnp.float32).astype(jnp.bfloat16)
    return (mixed_out, jnp.stack(ending_parts, axis=0))


def solution(mesh):
    placed = (
        P(("req", "seq"), None),
        P(("req", "seq"), None),
        P(("req", "seq"), None),
        P(("req", "seq"), None),
        P(),
        P(),
        P(),
        P(),
        P(),
        P(),
        P(),
        P(),
    )
    return jax.shard_map(
        per_device,
        mesh=mesh,
        in_specs=placed,
        out_specs=(P(("req", "seq"), None), P("req", "seq", None, None)),
        check_vma=False,
    )
```

```python
import jax
import jax.numpy as jnp
from jax import lax
from jax.sharding import PartitionSpec as P

N = 128
STRETCH = 256


def from_behind(value, axis, steps):
    count = lax.axis_size(axis)
    leading, last = (max(0, -steps), min(count, count - steps))
    return lax.ppermute(value, axis, [(source, source + steps) for source in range(leading, last)])


LMAX_CH = 16


def chain_flat(earlier, later):
    return (earlier[0] * later[0], later[0][:, None] * earlier[1] + later[1])


def carried_in(gain, state, window):
    groups = lax.axis_size("seq")
    heads = gain.shape[0]
    share = heads // groups
    cells = state.shape[1] * state.shape[2]
    packed = jnp.concatenate(
        [state.reshape(heads, cells), jnp.broadcast_to(gain[:, None], (heads, 128))], axis=1
    )
    mine = lax.all_to_all(packed, "seq", split_axis=0, concat_axis=0, tiled=True)
    mine = mine.reshape(groups, share, cells + 128)
    parts = [(mine[k, :, cells], mine[k, :, :cells]) for k in range(groups)]
    prefixes = [(jnp.ones((share,), jnp.float32), jnp.zeros((share, cells), jnp.float32))]
    for k in range(groups):
        prefixes.append(chain_flat(prefixes[-1], parts[k]))
    whole = prefixes[-1]
    reach = -(-window // groups)
    behind = from_behind(whole, "req", reach)
    for step in range(reach - 1, 0, -1):
        behind = chain_flat(behind, from_behind(whole, "req", step))
    incoming = jnp.stack([chain_flat(behind, prefixes[k])[1] for k in range(groups)], axis=0)
    incoming = lax.all_to_all(incoming, "seq", split_axis=0, concat_axis=0, tiled=True)
    return incoming.reshape(state.shape)


def stretch_flags(prompt_stretches, stretch_ids):
    firsts = jnp.cumsum(prompt_stretches) - prompt_stretches
    last_stretches = firsts + prompt_stretches - 1
    starts = jnp.any(stretch_ids[:, None] == firsts[None, :], axis=1)
    finals = jnp.any(stretch_ids[:, None] == last_stretches[None, :], axis=1)
    return (starts, finals)


def causal_conv(row_block, history, weight, conv_bias, starts):
    conv_span = weight.shape[0]
    length = row_block.shape[0]
    extended = jnp.concatenate([history, row_block], axis=0)
    in_stretch = jnp.arange(length, dtype=jnp.int32) % STRETCH
    start_rows = jnp.repeat(starts, STRETCH)
    running = conv_bias[None, :]
    for offset in range(conv_span):
        lag_rows = conv_span - 1 - offset
        shifted = extended[offset : offset + length].astype(jnp.float32)
        usable = jnp.logical_not((in_stretch < lag_rows) & start_rows)
        running = running + weight[offset][None, :] * jnp.where(usable[:, None], shifted, 0.0)
    return jax.nn.silu(running).astype(jnp.bfloat16)


def stretch_summary(x_stretch, bc_stretch, dt_stretch, dt_bias, a_log):
    state_size = bc_stretch.shape[1] // 2
    b_mat = bc_stretch[:, :state_size]
    step_size = jax.nn.softplus(dt_stretch.astype(jnp.float32) + dt_bias[None, :])
    log_decay = jnp.cumsum(-jnp.exp(a_log)[None, :] * step_size, axis=0)
    tail_weight = jnp.exp(log_decay[-1][None, :] - log_decay) * step_size
    weighted_x = (x_stretch.astype(jnp.float32) * tail_weight[:, :, None]).astype(jnp.bfloat16)
    stretch_state = jnp.einsum("uhp,un->hpn", weighted_x, b_mat, preferred_element_type=jnp.float32)
    return (step_size, log_decay, stretch_state)


def stretch_diag(x_stretch, bc_stretch, step_size, log_decay):
    state_size = bc_stretch.shape[1] // 2
    b_mat = bc_stretch[:, :state_size]
    c_mat = bc_stretch[:, state_size:]
    scores = jnp.dot(c_mat, b_mat.T, preferred_element_type=jnp.float32)
    stretch_len = scores.shape[0]
    causal = jnp.arange(stretch_len)[:, None] >= jnp.arange(stretch_len)[None, :]
    by_head = log_decay.T
    segment = by_head[:, :, None] - by_head[:, None, :]
    decay_mask = jnp.where(causal[None], jnp.exp(jnp.where(causal[None], segment, 0.0)), 0.0)
    mixing = (scores[None] * decay_mask * step_size.T[:, None, :]).astype(jnp.bfloat16)
    return jnp.einsum("htu,uhp->thp", mixing, x_stretch, preferred_element_type=jnp.float32)


def finish_stretch(y_diag, log_decay, state_in, x_stretch, c_mat, d_skip):
    state_low = state_in.astype(jnp.bfloat16)
    y_off = jnp.exp(log_decay)[:, :, None] * jnp.einsum(
        "tn,hpn->thp", c_mat, state_low, preferred_element_type=jnp.float32
    )
    mixed_rows = y_diag + y_off + d_skip[None, :, None] * x_stretch.astype(jnp.float32)
    return mixed_rows.reshape(mixed_rows.shape[0], -1).astype(jnp.bfloat16)


def gate_and_norm(mixed_rows, z_rows, norm_gain):
    gated_rows = mixed_rows.astype(jnp.float32) * jax.nn.silu(z_rows.astype(jnp.float32))
    inv_rms = lax.rsqrt(jnp.mean(gated_rows * gated_rows, axis=-1, keepdims=True) + 1e-05)
    return (gated_rows * inv_rms * norm_gain[None, :]).astype(jnp.bfloat16)


def chain_states(earlier, later):
    return (earlier[0] * later[0], later[0][:, None, None] * earlier[1] + later[1])


def per_device(
    x_in,
    bc_in,
    z_in,
    dt_raw,
    conv_weight,
    conv_bias,
    dt_bias,
    a_log,
    d_skip,
    norm_gain,
    w_out,
    prompt_stretches,
):
    n_req = lax.axis_size("req")
    n_seq = lax.axis_size("seq")
    tok_rows, inner_width = x_in.shape
    head_count = a_log.shape[0]
    head_dim = inner_width // head_count
    share = head_count // n_seq
    width = share * head_dim
    chunk = tok_rows // n_req
    bc_width = bc_in.shape[1]
    state_size = bc_width // 2
    conv_span = conv_weight.shape[0]
    group = lax.axis_index("seq")
    block = lax.axis_index("req")

    x_slabs = jnp.stack([x_in[:, g * width : (g + 1) * width] for g in range(n_seq)], axis=0)
    dt_slabs = jnp.stack([dt_raw[:, g * share : (g + 1) * share] for g in range(n_seq)], axis=0)
    quarter = bc_width // n_seq
    bc_slabs = jnp.stack(
        [bc_in[:, g * quarter : (g + 1) * quarter] for g in range(n_seq)], axis=0
    )
    outbound = jnp.concatenate([x_slabs, bc_slabs, dt_slabs], axis=2)
    outbound = outbound.reshape(n_seq * n_req, chunk, -1)
    inbound = lax.all_to_all(outbound, ("seq", "req"), 0, 0, tiled=True)
    inbound = inbound.reshape(n_seq * tok_rows, -1)
    x_rows = inbound[:, :width]
    bc_rows = inbound[:, width : width + quarter]
    dt_rows = inbound[:, width + quarter :]

    row_count = x_rows.shape[0]
    stretch_count = row_count // STRETCH
    stretch_ids = block * stretch_count + jnp.arange(stretch_count, dtype=jnp.int32)
    starts, finals = stretch_flags(prompt_stretches, stretch_ids)
    edge_x, edge_bc = from_behind(
        (x_rows[row_count - conv_span + 1 :], bc_rows[row_count - conv_span + 1 :]), "req", 1
    )
    weight_x = lax.dynamic_slice_in_dim(conv_weight, group * width, width, axis=1)
    bias_x = lax.dynamic_slice_in_dim(conv_bias, group * width, width, axis=0)
    conv_x = causal_conv(x_rows, edge_x, weight_x, bias_x, starts)
    weight_bc = lax.dynamic_slice_in_dim(conv_weight, inner_width + group * quarter, quarter, axis=1)
    bias_bc = lax.dynamic_slice_in_dim(conv_bias, inner_width + group * quarter, quarter, axis=0)
    conv_quarter = causal_conv(bc_rows, edge_bc, weight_bc, bias_bc, starts)
    gathered = lax.all_gather(conv_quarter, "seq", axis=0, tiled=False)
    conv_bc = jnp.concatenate([gathered[g] for g in range(n_seq)], axis=1)
    bias_dt = lax.dynamic_slice_in_dim(dt_bias, group * share, share)
    rate_log = lax.dynamic_slice_in_dim(a_log, group * share, share)
    skip = lax.dynamic_slice_in_dim(d_skip, group * share, share)

    x_heads = conv_x.reshape(stretch_count, STRETCH, share, head_dim)
    bcs = conv_bc.reshape(stretch_count, STRETCH, bc_width)
    b_mat = bcs[:, :, :state_size]
    c_mat = bcs[:, :, state_size:]
    dts = dt_rows.reshape(stretch_count, STRETCH, share)
    step_size = jax.nn.softplus(dts.astype(jnp.float32) + bias_dt[None, None, :])
    log_decay = jnp.cumsum(-jnp.exp(rate_log)[None, None, :] * step_size, axis=1)
    tail_weight = jnp.exp(log_decay[:, -1:, :] - log_decay) * step_size
    weighted_x = (x_heads.astype(jnp.float32) * tail_weight[..., None]).astype(jnp.bfloat16)
    stretch_state = jnp.einsum(
        "cuhp,cun->chpn", weighted_x, b_mat, preferred_element_type=jnp.float32
    )
    carried = jnp.where(starts[:, None], 0.0, jnp.exp(log_decay[:, -1, :]))
    total = (jnp.ones((share,), jnp.float32), jnp.zeros((share, head_dim, N), jnp.float32))
    for stretch in range(stretch_count):
        total = chain_states(total, (carried[stretch], stretch_state[stretch]))
    reach = -(-(LMAX_CH - 1) // stretch_count)
    behind = from_behind(total, "req", reach)
    for step in range(reach - 1, 0, -1):
        behind = chain_states(behind, from_behind(total, "req", step))
    state_prev = behind[1]

    scores = jnp.einsum("ctn,cun->ctu", c_mat, b_mat, preferred_element_type=jnp.float32)
    causal = jnp.arange(STRETCH)[:, None] >= jnp.arange(STRETCH)[None, :]
    by_head = log_decay.transpose(0, 2, 1)
    segment = by_head[:, :, :, None] - by_head[:, :, None, :]
    decay_mask = jnp.where(causal, jnp.exp(jnp.where(causal, segment, 0.0)), 0.0)
    mixing = (
        scores[:, None] * decay_mask * step_size.transpose(0, 2, 1)[:, :, None, :]
    ).astype(jnp.bfloat16)
    y_diag = jnp.einsum("chtu,cuhp->cthp", mixing, x_heads, preferred_element_type=jnp.float32)

    state_ins = []
    ending_parts = []
    for stretch in range(stretch_count):
        state_in = jnp.where(starts[stretch], jnp.zeros_like(state_prev), state_prev)
        state_ins.append(state_in)
        state_out = (
            jnp.exp(log_decay[stretch, -1])[:, None, None] * state_in + stretch_state[stretch]
        )
        ending_parts.append(jnp.where(finals[stretch], state_out, jnp.zeros_like(state_out)))
        state_prev = state_out
    state_low = jnp.stack(state_ins, axis=0).astype(jnp.bfloat16)
    state_low = state_low.reshape(stretch_count, width, N)
    y_off = jnp.repeat(jnp.exp(log_decay), head_dim, axis=-1) * jnp.einsum(
        "ctn,cqn->ctq", c_mat, state_low, preferred_element_type=jnp.float32
    )
    y_diag = jnp.concatenate(
        [
            jnp.einsum(
                "ctu,cup->ctp", mixing[:, h], x_heads[:, :, h], preferred_element_type=jnp.float32
            )
            for h in range(share)
        ],
        axis=-1,
    )
    x_flat = conv_x.reshape(stretch_count, STRETCH, width).astype(jnp.float32)
    mixed = y_diag + y_off + jnp.repeat(skip, head_dim)[None, None, :] * x_flat
    mixed = mixed.astype(jnp.bfloat16).reshape(n_seq * n_req, chunk, width)
    back = lax.all_to_all(mixed, ("seq", "req"), 0, 0, tiled=True)
    back = back.reshape(n_seq, tok_rows, width)
    mixed_tokens = jnp.concatenate([back[g] for g in range(n_seq)], axis=1)
    normed = gate_and_norm(mixed_tokens, z_in, norm_gain)
    mixed_out = jnp.dot(normed, w_out, preferred_element_type=jnp.float32).astype(jnp.bfloat16)
    return (mixed_out, jnp.stack(ending_parts, axis=0))


def solution(mesh):
    placed = (
        P(("req", "seq"), None),
        P(("req", "seq"), None),
        P(("req", "seq"), None),
        P(("req", "seq"), None),
        P(),
        P(),
        P(),
        P(),
        P(),
        P(),
        P(),
        P(),
    )
    return jax.shard_map(
        per_device,
        mesh=mesh,
        in_specs=placed,
        out_specs=(P(("req", "seq"), None), P("req", "seq", None, None)),
        check_vma=False,
    )
```

```python
import jax
import jax.numpy as jnp
from jax import lax
from jax.sharding import PartitionSpec as P

N = 128
STRETCH = 256


def from_behind(value, axis, steps):
    count = lax.axis_size(axis)
    leading, last = (max(0, -steps), min(count, count - steps))
    return lax.ppermute(value, axis, [(source, source + steps) for source in range(leading, last)])


LMAX_CH = 16


def chain_flat(earlier, later):
    return (earlier[0] * later[0], later[0][:, None] * earlier[1] + later[1])


def carried_in(gain, state, window):
    groups = lax.axis_size("seq")
    heads = gain.shape[0]
    share = heads // groups
    cells = state.shape[1] * state.shape[2]
    packed = jnp.concatenate(
        [state.reshape(heads, cells), jnp.broadcast_to(gain[:, None], (heads, 128))], axis=1
    )
    mine = lax.all_to_all(packed, "seq", split_axis=0, concat_axis=0, tiled=True)
    mine = mine.reshape(groups, share, cells + 128)
    parts = [(mine[k, :, cells], mine[k, :, :cells]) for k in range(groups)]
    prefixes = [(jnp.ones((share,), jnp.float32), jnp.zeros((share, cells), jnp.float32))]
    for k in range(groups):
        prefixes.append(chain_flat(prefixes[-1], parts[k]))
    whole = prefixes[-1]
    reach = -(-window // groups)
    behind = from_behind(whole, "req", reach)
    for step in range(reach - 1, 0, -1):
        behind = chain_flat(behind, from_behind(whole, "req", step))
    incoming = jnp.stack([chain_flat(behind, prefixes[k])[1] for k in range(groups)], axis=0)
    incoming = lax.all_to_all(incoming, "seq", split_axis=0, concat_axis=0, tiled=True)
    return incoming.reshape(state.shape)


def stretch_flags(prompt_stretches, stretch_ids):
    firsts = jnp.cumsum(prompt_stretches) - prompt_stretches
    last_stretches = firsts + prompt_stretches - 1
    starts = jnp.any(stretch_ids[:, None] == firsts[None, :], axis=1)
    finals = jnp.any(stretch_ids[:, None] == last_stretches[None, :], axis=1)
    return (starts, finals)


def causal_conv(row_block, history, weight, conv_bias, starts):
    conv_span = weight.shape[0]
    length = row_block.shape[0]
    extended = jnp.concatenate([history, row_block], axis=0)
    in_stretch = jnp.arange(length, dtype=jnp.int32) % STRETCH
    start_rows = jnp.repeat(starts, STRETCH)
    running = conv_bias[None, :]
    for offset in range(conv_span):
        lag_rows = conv_span - 1 - offset
        shifted = extended[offset : offset + length].astype(jnp.float32)
        usable = jnp.logical_not((in_stretch < lag_rows) & start_rows)
        running = running + weight[offset][None, :] * jnp.where(usable[:, None], shifted, 0.0)
    return jax.nn.silu(running).astype(jnp.bfloat16)


def stretch_summary(x_stretch, bc_stretch, dt_stretch, dt_bias, a_log):
    state_size = bc_stretch.shape[1] // 2
    b_mat = bc_stretch[:, :state_size]
    step_size = jax.nn.softplus(dt_stretch.astype(jnp.float32) + dt_bias[None, :])
    log_decay = jnp.cumsum(-jnp.exp(a_log)[None, :] * step_size, axis=0)
    tail_weight = jnp.exp(log_decay[-1][None, :] - log_decay) * step_size
    weighted_x = (x_stretch.astype(jnp.float32) * tail_weight[:, :, None]).astype(jnp.bfloat16)
    stretch_state = jnp.einsum("uhp,un->hpn", weighted_x, b_mat, preferred_element_type=jnp.float32)
    return (step_size, log_decay, stretch_state)


def stretch_diag(x_stretch, bc_stretch, step_size, log_decay):
    state_size = bc_stretch.shape[1] // 2
    b_mat = bc_stretch[:, :state_size]
    c_mat = bc_stretch[:, state_size:]
    scores = jnp.dot(c_mat, b_mat.T, preferred_element_type=jnp.float32)
    stretch_len = scores.shape[0]
    causal = jnp.arange(stretch_len)[:, None] >= jnp.arange(stretch_len)[None, :]
    by_head = log_decay.T
    segment = by_head[:, :, None] - by_head[:, None, :]
    decay_mask = jnp.where(causal[None], jnp.exp(jnp.where(causal[None], segment, 0.0)), 0.0)
    mixing = (scores[None] * decay_mask * step_size.T[:, None, :]).astype(jnp.bfloat16)
    return jnp.einsum("htu,uhp->thp", mixing, x_stretch, preferred_element_type=jnp.float32)


def finish_stretch(y_diag, log_decay, state_in, x_stretch, c_mat, d_skip):
    state_low = state_in.astype(jnp.bfloat16)
    y_off = jnp.exp(log_decay)[:, :, None] * jnp.einsum(
        "tn,hpn->thp", c_mat, state_low, preferred_element_type=jnp.float32
    )
    mixed_rows = y_diag + y_off + d_skip[None, :, None] * x_stretch.astype(jnp.float32)
    return mixed_rows.reshape(mixed_rows.shape[0], -1).astype(jnp.bfloat16)


def gate_and_norm(mixed_rows, z_rows, norm_gain):
    gated_rows = mixed_rows.astype(jnp.float32) * jax.nn.silu(z_rows.astype(jnp.float32))
    inv_rms = lax.rsqrt(jnp.mean(gated_rows * gated_rows, axis=-1, keepdims=True) + 1e-05)
    return (gated_rows * inv_rms * norm_gain[None, :]).astype(jnp.bfloat16)


def chain_states(earlier, later):
    return (earlier[0] * later[0], later[0][:, None, None] * earlier[1] + later[1])


def per_device(
    x_in,
    bc_in,
    z_in,
    dt_raw,
    conv_weight,
    conv_bias,
    dt_bias,
    a_log,
    d_skip,
    norm_gain,
    w_out,
    prompt_stretches,
):
    n_req = lax.axis_size("req")
    n_seq = lax.axis_size("seq")
    tok_rows, inner_width = x_in.shape
    head_count = a_log.shape[0]
    head_dim = inner_width // head_count
    share = head_count // n_seq
    width = share * head_dim
    chunk = tok_rows // n_req
    bc_width = bc_in.shape[1]
    state_size = bc_width // 2
    conv_span = conv_weight.shape[0]
    group = lax.axis_index("seq")
    block = lax.axis_index("req")

    x_slabs = jnp.stack([x_in[:, g * width : (g + 1) * width] for g in range(n_seq)], axis=0)
    dt_slabs = jnp.stack([dt_raw[:, g * share : (g + 1) * share] for g in range(n_seq)], axis=0)
    bc_slabs = jnp.broadcast_to(bc_in[None], (n_seq, tok_rows, bc_width))
    outbound = jnp.concatenate([x_slabs, bc_slabs, dt_slabs], axis=2)
    outbound = outbound.reshape(n_seq * n_req, chunk, -1)
    inbound = lax.all_to_all(outbound, ("seq", "req"), 0, 0, tiled=True)
    inbound = inbound.reshape(n_seq * tok_rows, -1)
    x_rows = inbound[:, :width]
    bc_rows = inbound[:, width : width + bc_width]
    dt_rows = inbound[:, width + bc_width :]

    row_count = x_rows.shape[0]
    stretch_count = row_count // STRETCH
    stretch_ids = block * stretch_count + jnp.arange(stretch_count, dtype=jnp.int32)
    starts, finals = stretch_flags(prompt_stretches, stretch_ids)
    edge_x, edge_bc = from_behind(
        (x_rows[row_count - conv_span + 1 :], bc_rows[row_count - conv_span + 1 :]), "req", 1
    )
    weight_x = lax.dynamic_slice_in_dim(conv_weight, group * width, width, axis=1)
    bias_x = lax.dynamic_slice_in_dim(conv_bias, group * width, width, axis=0)
    conv_x = causal_conv(x_rows, edge_x, weight_x, bias_x, starts)
    conv_bc = causal_conv(
        bc_rows, edge_bc, conv_weight[:, inner_width:], conv_bias[inner_width:], starts
    )
    bias_dt = lax.dynamic_slice_in_dim(dt_bias, group * share, share)
    rate_log = lax.dynamic_slice_in_dim(a_log, group * share, share)
    skip = lax.dynamic_slice_in_dim(d_skip, group * share, share)

    x_heads = conv_x.reshape(stretch_count, STRETCH, share, head_dim)
    bcs = conv_bc.reshape(stretch_count, STRETCH, bc_width)
    b_mat = bcs[:, :, :state_size]
    c_mat = bcs[:, :, state_size:]
    dts = dt_rows.reshape(stretch_count, STRETCH, share)
    step_size = jax.nn.softplus(dts.astype(jnp.float32) + bias_dt[None, None, :])
    log_decay = jnp.cumsum(-jnp.exp(rate_log)[None, None, :] * step_size, axis=1)
    tail_weight = jnp.exp(log_decay[:, -1:, :] - log_decay) * step_size
    weighted_x = (x_heads.astype(jnp.float32) * tail_weight[..., None]).astype(jnp.bfloat16)
    stretch_state = jnp.einsum(
        "cuhp,cun->chpn", weighted_x, b_mat, preferred_element_type=jnp.float32
    )
    carried = jnp.where(starts[:, None], 0.0, jnp.exp(log_decay[:, -1, :]))
    total = (jnp.ones((share,), jnp.float32), jnp.zeros((share, head_dim, N), jnp.float32))
    for stretch in range(stretch_count):
        total = chain_states(total, (carried[stretch], stretch_state[stretch]))
    reach = -(-(LMAX_CH - 1) // stretch_count)
    behind = from_behind(total, "req", reach)
    for step in range(reach - 1, 0, -1):
        behind = chain_states(behind, from_behind(total, "req", step))
    state_prev = behind[1]

    scores = jnp.einsum("ctn,cun->ctu", c_mat, b_mat, preferred_element_type=jnp.float32)
    causal = jnp.arange(STRETCH)[:, None] >= jnp.arange(STRETCH)[None, :]
    by_head = log_decay.transpose(0, 2, 1)
    segment = by_head[:, :, :, None] - by_head[:, :, None, :]
    decay_mask = jnp.where(causal, jnp.exp(jnp.where(causal, segment, 0.0)), 0.0)
    mixing = (
        scores[:, None] * decay_mask * step_size.transpose(0, 2, 1)[:, :, None, :]
    ).astype(jnp.bfloat16)
    y_diag = jnp.einsum("chtu,cuhp->cthp", mixing, x_heads, preferred_element_type=jnp.float32)

    keep = jnp.where(starts, 0.0, 1.0)
    gains = jnp.exp(log_decay[:, -1, :])
    c_idx = jnp.arange(stretch_count)[:, None, None]
    k_idx = jnp.arange(-1, stretch_count)[None, :, None]
    m_idx = jnp.arange(stretch_count)[None, None, :]
    keep_span = (m_idx > k_idx) & (m_idx <= c_idx)
    gain_span = (m_idx > k_idx) & (m_idx < c_idx)
    live = k_idx < c_idx
    factors = jnp.where(keep_span[..., None], keep[None, None, :, None], 1.0) * jnp.where(
        gain_span[..., None], gains[None, None, :, :], 1.0
    )
    weights = jnp.where(live, jnp.prod(factors, axis=2), 0.0)
    sources = jnp.concatenate([state_prev[None], stretch_state], axis=0)
    state_in_all = jnp.sum(weights[:, :, :, None, None] * sources[None], axis=1)
    state_out_all = gains[:, :, None, None] * state_in_all + stretch_state
    endings = jnp.where(finals[:, None, None, None], state_out_all, 0.0)
    state_ins = [state_in_all[c] for c in range(stretch_count)]
    state_low = jnp.stack(state_ins, axis=0).astype(jnp.bfloat16)
    state_low = state_low.reshape(stretch_count, width, N)
    y_off = jnp.repeat(jnp.exp(log_decay), head_dim, axis=-1) * jnp.einsum(
        "ctn,cqn->ctq", c_mat, state_low, preferred_element_type=jnp.float32
    )
    y_diag = jnp.concatenate(
        [
            jnp.einsum(
                "ctu,cup->ctp", mixing[:, h], x_heads[:, :, h], preferred_element_type=jnp.float32
            )
            for h in range(share)
        ],
        axis=-1,
    )
    x_flat = conv_x.reshape(stretch_count, STRETCH, width).astype(jnp.float32)
    mixed = y_diag + y_off + jnp.repeat(skip, head_dim)[None, None, :] * x_flat
    mixed = mixed.astype(jnp.bfloat16).reshape(n_seq * n_req, chunk, width)
    back = lax.all_to_all(mixed, ("seq", "req"), 0, 0, tiled=True)
    back = back.reshape(n_seq, tok_rows, width)
    mixed_tokens = jnp.concatenate([back[g] for g in range(n_seq)], axis=1)
    normed = gate_and_norm(mixed_tokens, z_in, norm_gain)
    mixed_out = jnp.dot(normed, w_out, preferred_element_type=jnp.float32).astype(jnp.bfloat16)
    return (mixed_out, endings)


def solution(mesh):
    placed = (
        P(("req", "seq"), None),
        P(("req", "seq"), None),
        P(("req", "seq"), None),
        P(("req", "seq"), None),
        P(),
        P(),
        P(),
        P(),
        P(),
        P(),
        P(),
        P(),
    )
    return jax.shard_map(
        per_device,
        mesh=mesh,
        in_specs=placed,
        out_specs=(P(("req", "seq"), None), P("req", "seq", None, None)),
        check_vma=False,
    )
```

```python
import jax
import jax.numpy as jnp
from jax import lax
from jax.sharding import PartitionSpec as P

N = 128
STRETCH = 256


def from_behind(value, axis, steps):
    count = lax.axis_size(axis)
    leading, last = (max(0, -steps), min(count, count - steps))
    return lax.ppermute(value, axis, [(source, source + steps) for source in range(leading, last)])


LMAX_CH = 16


def chain_flat(earlier, later):
    return (earlier[0] * later[0], later[0][:, None] * earlier[1] + later[1])


def carried_in(gain, state, window):
    groups = lax.axis_size("seq")
    heads = gain.shape[0]
    share = heads // groups
    cells = state.shape[1] * state.shape[2]
    packed = jnp.concatenate(
        [state.reshape(heads, cells), jnp.broadcast_to(gain[:, None], (heads, 128))], axis=1
    )
    mine = lax.all_to_all(packed, "seq", split_axis=0, concat_axis=0, tiled=True)
    mine = mine.reshape(groups, share, cells + 128)
    parts = [(mine[k, :, cells], mine[k, :, :cells]) for k in range(groups)]
    prefixes = [(jnp.ones((share,), jnp.float32), jnp.zeros((share, cells), jnp.float32))]
    for k in range(groups):
        prefixes.append(chain_flat(prefixes[-1], parts[k]))
    whole = prefixes[-1]
    reach = -(-window // groups)
    behind = from_behind(whole, "req", reach)
    for step in range(reach - 1, 0, -1):
        behind = chain_flat(behind, from_behind(whole, "req", step))
    incoming = jnp.stack([chain_flat(behind, prefixes[k])[1] for k in range(groups)], axis=0)
    incoming = lax.all_to_all(incoming, "seq", split_axis=0, concat_axis=0, tiled=True)
    return incoming.reshape(state.shape)


def stretch_flags(prompt_stretches, stretch_ids):
    firsts = jnp.cumsum(prompt_stretches) - prompt_stretches
    last_stretches = firsts + prompt_stretches - 1
    starts = jnp.any(stretch_ids[:, None] == firsts[None, :], axis=1)
    finals = jnp.any(stretch_ids[:, None] == last_stretches[None, :], axis=1)
    return (starts, finals)


def causal_conv(row_block, history, weight, conv_bias, starts):
    conv_span = weight.shape[0]
    length = row_block.shape[0]
    extended = jnp.concatenate([history, row_block], axis=0)
    in_stretch = jnp.arange(length, dtype=jnp.int32) % STRETCH
    start_rows = jnp.repeat(starts, STRETCH)
    running = conv_bias[None, :]
    for offset in range(conv_span):
        lag_rows = conv_span - 1 - offset
        shifted = extended[offset : offset + length].astype(jnp.float32)
        usable = jnp.logical_not((in_stretch < lag_rows) & start_rows)
        running = running + weight[offset][None, :] * jnp.where(usable[:, None], shifted, 0.0)
    return jax.nn.silu(running).astype(jnp.bfloat16)


def stretch_summary(x_stretch, bc_stretch, dt_stretch, dt_bias, a_log):
    state_size = bc_stretch.shape[1] // 2
    b_mat = bc_stretch[:, :state_size]
    step_size = jax.nn.softplus(dt_stretch.astype(jnp.float32) + dt_bias[None, :])
    log_decay = jnp.cumsum(-jnp.exp(a_log)[None, :] * step_size, axis=0)
    tail_weight = jnp.exp(log_decay[-1][None, :] - log_decay) * step_size
    weighted_x = (x_stretch.astype(jnp.float32) * tail_weight[:, :, None]).astype(jnp.bfloat16)
    stretch_state = jnp.einsum("uhp,un->hpn", weighted_x, b_mat, preferred_element_type=jnp.float32)
    return (step_size, log_decay, stretch_state)


def stretch_diag(x_stretch, bc_stretch, step_size, log_decay):
    state_size = bc_stretch.shape[1] // 2
    b_mat = bc_stretch[:, :state_size]
    c_mat = bc_stretch[:, state_size:]
    scores = jnp.dot(c_mat, b_mat.T, preferred_element_type=jnp.float32)
    stretch_len = scores.shape[0]
    causal = jnp.arange(stretch_len)[:, None] >= jnp.arange(stretch_len)[None, :]
    by_head = log_decay.T
    segment = by_head[:, :, None] - by_head[:, None, :]
    decay_mask = jnp.where(causal[None], jnp.exp(jnp.where(causal[None], segment, 0.0)), 0.0)
    mixing = (scores[None] * decay_mask * step_size.T[:, None, :]).astype(jnp.bfloat16)
    return jnp.einsum("htu,uhp->thp", mixing, x_stretch, preferred_element_type=jnp.float32)


def finish_stretch(y_diag, log_decay, state_in, x_stretch, c_mat, d_skip):
    state_low = state_in.astype(jnp.bfloat16)
    y_off = jnp.exp(log_decay)[:, :, None] * jnp.einsum(
        "tn,hpn->thp", c_mat, state_low, preferred_element_type=jnp.float32
    )
    mixed_rows = y_diag + y_off + d_skip[None, :, None] * x_stretch.astype(jnp.float32)
    return mixed_rows.reshape(mixed_rows.shape[0], -1).astype(jnp.bfloat16)


def gate_and_norm(mixed_rows, z_rows, norm_gain):
    gated_rows = mixed_rows.astype(jnp.float32) * jax.nn.silu(z_rows.astype(jnp.float32))
    inv_rms = lax.rsqrt(jnp.mean(gated_rows * gated_rows, axis=-1, keepdims=True) + 1e-05)
    return (gated_rows * inv_rms * norm_gain[None, :]).astype(jnp.bfloat16)


def chain_states(earlier, later):
    return (earlier[0] * later[0], later[0][:, None, None] * earlier[1] + later[1])


def per_device(
    x_in,
    bc_in,
    z_in,
    dt_raw,
    conv_weight,
    conv_bias,
    dt_bias,
    a_log,
    d_skip,
    norm_gain,
    w_out,
    prompt_stretches,
):
    n_req = lax.axis_size("req")
    n_seq = lax.axis_size("seq")
    tok_rows, inner_width = x_in.shape
    head_count = a_log.shape[0]
    head_dim = inner_width // head_count
    share = head_count // n_seq
    width = share * head_dim
    chunk = tok_rows // n_req
    bc_width = bc_in.shape[1]
    state_size = bc_width // 2
    conv_span = conv_weight.shape[0]
    group = lax.axis_index("seq")
    block = lax.axis_index("req")

    x_slabs = jnp.stack([x_in[:, g * width : (g + 1) * width] for g in range(n_seq)], axis=0)
    dt_slabs = jnp.stack([dt_raw[:, g * share : (g + 1) * share] for g in range(n_seq)], axis=0)
    bc_slabs = jnp.broadcast_to(bc_in[None], (n_seq, tok_rows, bc_width))
    outbound = jnp.concatenate([x_slabs, bc_slabs, dt_slabs], axis=2)
    outbound = outbound.reshape(n_seq * n_req, chunk, -1)
    inbound = lax.all_to_all(outbound, ("seq", "req"), 0, 0, tiled=True)
    inbound = inbound.reshape(n_seq * tok_rows, -1)
    x_rows = inbound[:, :width]
    bc_rows = inbound[:, width : width + bc_width]
    dt_rows = inbound[:, width + bc_width :]

    row_count = x_rows.shape[0]
    stretch_count = row_count // STRETCH
    stretch_ids = block * stretch_count + jnp.arange(stretch_count, dtype=jnp.int32)
    starts, finals = stretch_flags(prompt_stretches, stretch_ids)
    edge_x, edge_bc = from_behind(
        (x_rows[row_count - conv_span + 1 :], bc_rows[row_count - conv_span + 1 :]), "req", 1
    )
    weight_x = lax.dynamic_slice_in_dim(conv_weight, group * width, width, axis=1)
    bias_x = lax.dynamic_slice_in_dim(conv_bias, group * width, width, axis=0)
    conv_x = causal_conv(x_rows, edge_x, weight_x, bias_x, starts)
    conv_bc = causal_conv(
        bc_rows, edge_bc, conv_weight[:, inner_width:], conv_bias[inner_width:], starts
    )
    bias_dt = lax.dynamic_slice_in_dim(dt_bias, group * share, share)
    rate_log = lax.dynamic_slice_in_dim(a_log, group * share, share)
    skip = lax.dynamic_slice_in_dim(d_skip, group * share, share)

    x_heads = conv_x.reshape(stretch_count, STRETCH, share, head_dim)
    bcs = conv_bc.reshape(stretch_count, STRETCH, bc_width)
    b_mat = bcs[:, :, :state_size]
    c_mat = bcs[:, :, state_size:]
    dts = dt_rows.reshape(stretch_count, STRETCH, share)
    step_size = jax.nn.softplus(dts.astype(jnp.float32) + bias_dt[None, None, :])
    rates = -jnp.exp(rate_log)[None, None, :] * step_size
    lower = (jnp.arange(STRETCH)[:, None] >= jnp.arange(STRETCH)[None, :]).astype(jnp.float32)
    log_decay = jnp.einsum(
        "tu,cuh->cth", lower, rates, precision=lax.Precision.HIGHEST,
        preferred_element_type=jnp.float32,
    )
    tail_weight = jnp.exp(log_decay[:, -1:, :] - log_decay) * step_size
    weighted_x = (x_heads.astype(jnp.float32) * tail_weight[..., None]).astype(jnp.bfloat16)
    stretch_state = jnp.einsum(
        "cuhp,cun->chpn", weighted_x, b_mat, preferred_element_type=jnp.float32
    )
    carried = jnp.where(starts[:, None], 0.0, jnp.exp(log_decay[:, -1, :]))
    total = (jnp.ones((share,), jnp.float32), jnp.zeros((share, head_dim, N), jnp.float32))
    for stretch in range(stretch_count):
        total = chain_states(total, (carried[stretch], stretch_state[stretch]))
    reach = -(-(LMAX_CH - 1) // stretch_count)
    behind = from_behind(total, "req", reach)
    for step in range(reach - 1, 0, -1):
        behind = chain_states(behind, from_behind(total, "req", step))
    state_prev = behind[1]

    scores = jnp.einsum("ctn,cun->ctu", c_mat, b_mat, preferred_element_type=jnp.float32)
    causal = jnp.arange(STRETCH)[:, None] >= jnp.arange(STRETCH)[None, :]
    by_head = log_decay.transpose(0, 2, 1)
    segment = by_head[:, :, :, None] - by_head[:, :, None, :]
    decay_mask = jnp.where(causal, jnp.exp(jnp.where(causal, segment, 0.0)), 0.0)
    mixing = (
        scores[:, None] * decay_mask * step_size.transpose(0, 2, 1)[:, :, None, :]
    ).astype(jnp.bfloat16)

    keep = jnp.where(starts, 0.0, 1.0)
    gains = jnp.exp(log_decay[:, -1, :])
    c_idx = jnp.arange(stretch_count)[:, None, None]
    k_idx = jnp.arange(-1, stretch_count)[None, :, None]
    m_idx = jnp.arange(stretch_count)[None, None, :]
    keep_span = (m_idx > k_idx) & (m_idx <= c_idx)
    gain_span = (m_idx > k_idx) & (m_idx < c_idx)
    live = k_idx < c_idx
    factors = jnp.where(keep_span[..., None], keep[None, None, :, None], 1.0) * jnp.where(
        gain_span[..., None], gains[None, None, :, :], 1.0
    )
    weights = jnp.where(live, jnp.prod(factors, axis=2), 0.0)
    sources = jnp.concatenate([state_prev[None], stretch_state], axis=0)
    state_in_all = jnp.sum(weights[:, :, :, None, None] * sources[None], axis=1)
    state_out_all = gains[:, :, None, None] * state_in_all + stretch_state
    endings = jnp.where(finals[:, None, None, None], state_out_all, 0.0)
    state_ins = [state_in_all[c] for c in range(stretch_count)]
    state_low = jnp.stack(state_ins, axis=0).astype(jnp.bfloat16)
    state_low = state_low.reshape(stretch_count, width, N)
    y_off = jnp.repeat(jnp.exp(log_decay), head_dim, axis=-1) * jnp.einsum(
        "ctn,cqn->ctq", c_mat, state_low, preferred_element_type=jnp.float32
    )
    y_diag = jnp.concatenate(
        [
            jnp.einsum(
                "ctu,cup->ctp", mixing[:, h], x_heads[:, :, h], preferred_element_type=jnp.float32
            )
            for h in range(share)
        ],
        axis=-1,
    )
    x_flat = conv_x.reshape(stretch_count, STRETCH, width).astype(jnp.float32)
    mixed = y_diag + y_off + jnp.repeat(skip, head_dim)[None, None, :] * x_flat
    mixed = mixed.astype(jnp.bfloat16).reshape(n_seq * n_req, chunk, width)
    back = lax.all_to_all(mixed, ("seq", "req"), 0, 0, tiled=True)
    back = back.reshape(n_seq, tok_rows, width)
    mixed_tokens = jnp.concatenate([back[g] for g in range(n_seq)], axis=1)
    normed = gate_and_norm(mixed_tokens, z_in, norm_gain)
    mixed_out = jnp.dot(normed, w_out, preferred_element_type=jnp.float32).astype(jnp.bfloat16)
    return (mixed_out, endings)


def solution(mesh):
    placed = (
        P(("req", "seq"), None),
        P(("req", "seq"), None),
        P(("req", "seq"), None),
        P(("req", "seq"), None),
        P(),
        P(),
        P(),
        P(),
        P(),
        P(),
        P(),
        P(),
    )
    return jax.shard_map(
        per_device,
        mesh=mesh,
        in_specs=placed,
        out_specs=(P(("req", "seq"), None), P("req", "seq", None, None)),
        check_vma=False,
    )
```

```python
import jax
import jax.numpy as jnp
from jax import lax
from jax.sharding import PartitionSpec as P

N = 128
STRETCH = 256


def from_behind(value, axis, steps):
    count = lax.axis_size(axis)
    leading, last = (max(0, -steps), min(count, count - steps))
    return lax.ppermute(value, axis, [(source, source + steps) for source in range(leading, last)])


LMAX_CH = 16


def chain_flat(earlier, later):
    return (earlier[0] * later[0], later[0][:, None] * earlier[1] + later[1])


def carried_in(gain, state, window):
    groups = lax.axis_size("seq")
    heads = gain.shape[0]
    share = heads // groups
    cells = state.shape[1] * state.shape[2]
    packed = jnp.concatenate(
        [state.reshape(heads, cells), jnp.broadcast_to(gain[:, None], (heads, 128))], axis=1
    )
    mine = lax.all_to_all(packed, "seq", split_axis=0, concat_axis=0, tiled=True)
    mine = mine.reshape(groups, share, cells + 128)
    parts = [(mine[k, :, cells], mine[k, :, :cells]) for k in range(groups)]
    prefixes = [(jnp.ones((share,), jnp.float32), jnp.zeros((share, cells), jnp.float32))]
    for k in range(groups):
        prefixes.append(chain_flat(prefixes[-1], parts[k]))
    whole = prefixes[-1]
    reach = -(-window // groups)
    behind = from_behind(whole, "req", reach)
    for step in range(reach - 1, 0, -1):
        behind = chain_flat(behind, from_behind(whole, "req", step))
    incoming = jnp.stack([chain_flat(behind, prefixes[k])[1] for k in range(groups)], axis=0)
    incoming = lax.all_to_all(incoming, "seq", split_axis=0, concat_axis=0, tiled=True)
    return incoming.reshape(state.shape)


def stretch_flags(prompt_stretches, stretch_ids):
    firsts = jnp.cumsum(prompt_stretches) - prompt_stretches
    last_stretches = firsts + prompt_stretches - 1
    starts = jnp.any(stretch_ids[:, None] == firsts[None, :], axis=1)
    finals = jnp.any(stretch_ids[:, None] == last_stretches[None, :], axis=1)
    return (starts, finals)


def causal_conv(row_block, history, weight, conv_bias, starts):
    conv_span = weight.shape[0]
    length = row_block.shape[0]
    extended = jnp.concatenate([history, row_block], axis=0)
    in_stretch = jnp.arange(length, dtype=jnp.int32) % STRETCH
    start_rows = jnp.repeat(starts, STRETCH)
    running = conv_bias[None, :]
    for offset in range(conv_span):
        lag_rows = conv_span - 1 - offset
        shifted = extended[offset : offset + length].astype(jnp.float32)
        usable = jnp.logical_not((in_stretch < lag_rows) & start_rows)
        running = running + weight[offset][None, :] * jnp.where(usable[:, None], shifted, 0.0)
    return jax.nn.silu(running).astype(jnp.bfloat16)


def stretch_summary(x_stretch, bc_stretch, dt_stretch, dt_bias, a_log):
    state_size = bc_stretch.shape[1] // 2
    b_mat = bc_stretch[:, :state_size]
    step_size = jax.nn.softplus(dt_stretch.astype(jnp.float32) + dt_bias[None, :])
    log_decay = jnp.cumsum(-jnp.exp(a_log)[None, :] * step_size, axis=0)
    tail_weight = jnp.exp(log_decay[-1][None, :] - log_decay) * step_size
    weighted_x = (x_stretch.astype(jnp.float32) * tail_weight[:, :, None]).astype(jnp.bfloat16)
    stretch_state = jnp.einsum("uhp,un->hpn", weighted_x, b_mat, preferred_element_type=jnp.float32)
    return (step_size, log_decay, stretch_state)


def stretch_diag(x_stretch, bc_stretch, step_size, log_decay):
    state_size = bc_stretch.shape[1] // 2
    b_mat = bc_stretch[:, :state_size]
    c_mat = bc_stretch[:, state_size:]
    scores = jnp.dot(c_mat, b_mat.T, preferred_element_type=jnp.float32)
    stretch_len = scores.shape[0]
    causal = jnp.arange(stretch_len)[:, None] >= jnp.arange(stretch_len)[None, :]
    by_head = log_decay.T
    segment = by_head[:, :, None] - by_head[:, None, :]
    decay_mask = jnp.where(causal[None], jnp.exp(jnp.where(causal[None], segment, 0.0)), 0.0)
    mixing = (scores[None] * decay_mask * step_size.T[:, None, :]).astype(jnp.bfloat16)
    return jnp.einsum("htu,uhp->thp", mixing, x_stretch, preferred_element_type=jnp.float32)


def finish_stretch(y_diag, log_decay, state_in, x_stretch, c_mat, d_skip):
    state_low = state_in.astype(jnp.bfloat16)
    y_off = jnp.exp(log_decay)[:, :, None] * jnp.einsum(
        "tn,hpn->thp", c_mat, state_low, preferred_element_type=jnp.float32
    )
    mixed_rows = y_diag + y_off + d_skip[None, :, None] * x_stretch.astype(jnp.float32)
    return mixed_rows.reshape(mixed_rows.shape[0], -1).astype(jnp.bfloat16)


def gate_and_norm(mixed_rows, z_rows, norm_gain):
    gated_rows = mixed_rows.astype(jnp.float32) * jax.nn.silu(z_rows.astype(jnp.float32))
    inv_rms = lax.rsqrt(jnp.mean(gated_rows * gated_rows, axis=-1, keepdims=True) + 1e-05)
    return (gated_rows * inv_rms * norm_gain[None, :]).astype(jnp.bfloat16)


def chain_states(earlier, later):
    return (earlier[0] * later[0], later[0][:, None, None] * earlier[1] + later[1])


def per_device(
    x_in,
    bc_in,
    z_in,
    dt_raw,
    conv_weight,
    conv_bias,
    dt_bias,
    a_log,
    d_skip,
    norm_gain,
    w_out,
    prompt_stretches,
):
    n_req = lax.axis_size("req")
    n_seq = lax.axis_size("seq")
    tok_rows, inner_width = x_in.shape
    head_count = a_log.shape[0]
    head_dim = inner_width // head_count
    share = head_count // n_seq
    width = share * head_dim
    chunk = tok_rows // n_req
    bc_width = bc_in.shape[1]
    state_size = bc_width // 2
    conv_span = conv_weight.shape[0]
    group = lax.axis_index("seq")
    block = lax.axis_index("req")

    x_slabs = jnp.stack([x_in[:, g * width : (g + 1) * width] for g in range(n_seq)], axis=0)
    dt_slabs = jnp.stack([dt_raw[:, g * share : (g + 1) * share] for g in range(n_seq)], axis=0)
    bc_slabs = jnp.broadcast_to(bc_in[None], (n_seq, tok_rows, bc_width))
    outbound = jnp.concatenate([x_slabs, bc_slabs, dt_slabs], axis=2)
    outbound = outbound.reshape(n_seq * n_req, chunk, -1)
    inbound = lax.all_to_all(outbound, ("seq", "req"), 0, 0, tiled=True)
    inbound = inbound.reshape(n_seq * tok_rows, -1)
    x_rows = inbound[:, :width]
    bc_rows = inbound[:, width : width + bc_width]
    dt_rows = inbound[:, width + bc_width :]

    row_count = x_rows.shape[0]
    stretch_count = row_count // STRETCH
    stretch_ids = block * stretch_count + jnp.arange(stretch_count, dtype=jnp.int32)
    starts, finals = stretch_flags(prompt_stretches, stretch_ids)
    edge = from_behind(inbound[row_count - conv_span + 1 :, : width + bc_width], "req", 1)
    edge_x = edge[:, :width]
    edge_bc = edge[:, width:]
    weight_x = lax.dynamic_slice_in_dim(conv_weight, group * width, width, axis=1)
    bias_x = lax.dynamic_slice_in_dim(conv_bias, group * width, width, axis=0)
    conv_x = causal_conv(x_rows, edge_x, weight_x, bias_x, starts)
    conv_bc = causal_conv(
        bc_rows, edge_bc, conv_weight[:, inner_width:], conv_bias[inner_width:], starts
    )
    bias_dt = lax.dynamic_slice_in_dim(dt_bias, group * share, share)
    rate_log = lax.dynamic_slice_in_dim(a_log, group * share, share)
    skip = lax.dynamic_slice_in_dim(d_skip, group * share, share)

    x_heads = conv_x.reshape(stretch_count, STRETCH, share, head_dim)
    bcs = conv_bc.reshape(stretch_count, STRETCH, bc_width)
    b_mat = bcs[:, :, :state_size]
    c_mat = bcs[:, :, state_size:]
    dts = dt_rows.reshape(stretch_count, STRETCH, share)
    step_size = jax.nn.softplus(dts.astype(jnp.float32) + bias_dt[None, None, :])
    rates = -jnp.exp(rate_log)[None, None, :] * step_size
    lower = (jnp.arange(STRETCH)[:, None] >= jnp.arange(STRETCH)[None, :]).astype(jnp.float32)
    log_decay = jnp.einsum(
        "tu,cuh->cth", lower, rates, precision=lax.Precision.HIGHEST,
        preferred_element_type=jnp.float32,
    )
    tail_weight = jnp.exp(log_decay[:, -1:, :] - log_decay) * step_size
    weighted_x = (x_heads.astype(jnp.float32) * tail_weight[..., None]).astype(jnp.bfloat16)
    stretch_state = jnp.einsum(
        "cuhp,cun->chpn", weighted_x, b_mat, preferred_element_type=jnp.float32
    )
    carried = jnp.where(starts[:, None], 0.0, jnp.exp(log_decay[:, -1, :]))
    total = (jnp.ones((share,), jnp.float32), jnp.zeros((share, head_dim, N), jnp.float32))
    for stretch in range(stretch_count):
        total = chain_states(total, (carried[stretch], stretch_state[stretch]))
    reach = -(-(LMAX_CH - 1) // stretch_count)
    cells = head_dim * N
    packed = jnp.concatenate(
        [total[1].reshape(share, cells), jnp.broadcast_to(total[0][:, None], (share, 128))],
        axis=1,
    )

    def unpack(moved):
        return (moved[:, cells], moved[:, :cells].reshape(share, head_dim, N))

    behind = unpack(from_behind(packed, "req", reach))
    for step in range(reach - 1, 0, -1):
        behind = chain_states(behind, unpack(from_behind(packed, "req", step)))
    state_prev = behind[1]

    scores = jnp.einsum("ctn,cun->ctu", c_mat, b_mat, preferred_element_type=jnp.float32)
    causal = jnp.arange(STRETCH)[:, None] >= jnp.arange(STRETCH)[None, :]
    by_head = log_decay.transpose(0, 2, 1)
    segment = by_head[:, :, :, None] - by_head[:, :, None, :]
    decay_mask = jnp.where(causal, jnp.exp(jnp.where(causal, segment, 0.0)), 0.0)
    mixing = (
        scores[:, None] * decay_mask * step_size.transpose(0, 2, 1)[:, :, None, :]
    ).astype(jnp.bfloat16)

    keep = jnp.where(starts, 0.0, 1.0)
    gains = jnp.exp(log_decay[:, -1, :])
    c_idx = jnp.arange(stretch_count)[:, None, None]
    k_idx = jnp.arange(-1, stretch_count)[None, :, None]
    m_idx = jnp.arange(stretch_count)[None, None, :]
    keep_span = (m_idx > k_idx) & (m_idx <= c_idx)
    gain_span = (m_idx > k_idx) & (m_idx < c_idx)
    live = k_idx < c_idx
    factors = jnp.where(keep_span[..., None], keep[None, None, :, None], 1.0) * jnp.where(
        gain_span[..., None], gains[None, None, :, :], 1.0
    )
    weights = jnp.where(live, jnp.prod(factors, axis=2), 0.0)
    sources = jnp.concatenate([state_prev[None], stretch_state], axis=0)
    state_in_all = jnp.sum(weights[:, :, :, None, None] * sources[None], axis=1)
    state_out_all = gains[:, :, None, None] * state_in_all + stretch_state
    endings = jnp.where(finals[:, None, None, None], state_out_all, 0.0)
    state_ins = [state_in_all[c] for c in range(stretch_count)]
    state_low = jnp.stack(state_ins, axis=0).astype(jnp.bfloat16)
    state_low = state_low.reshape(stretch_count, width, N)
    y_off = jnp.repeat(jnp.exp(log_decay), head_dim, axis=-1) * jnp.einsum(
        "ctn,cqn->ctq", c_mat, state_low, preferred_element_type=jnp.float32
    )
    y_diag = jnp.concatenate(
        [
            jnp.einsum(
                "ctu,cup->ctp", mixing[:, h], x_heads[:, :, h], preferred_element_type=jnp.float32
            )
            for h in range(share)
        ],
        axis=-1,
    )
    x_flat = conv_x.reshape(stretch_count, STRETCH, width).astype(jnp.float32)
    mixed = y_diag + y_off + jnp.repeat(skip, head_dim)[None, None, :] * x_flat
    mixed = mixed.astype(jnp.bfloat16).reshape(n_seq * n_req, chunk, width)
    back = lax.all_to_all(mixed, ("seq", "req"), 0, 0, tiled=True)
    back = back.reshape(n_seq, tok_rows, width)
    mixed_tokens = jnp.concatenate([back[g] for g in range(n_seq)], axis=1)
    normed = gate_and_norm(mixed_tokens, z_in, norm_gain)
    mixed_out = jnp.dot(normed, w_out, preferred_element_type=jnp.float32).astype(jnp.bfloat16)
    return (mixed_out, endings)


def solution(mesh):
    placed = (
        P(("req", "seq"), None),
        P(("req", "seq"), None),
        P(("req", "seq"), None),
        P(("req", "seq"), None),
        P(),
        P(),
        P(),
        P(),
        P(),
        P(),
        P(),
        P(),
    )
    return jax.shard_map(
        per_device,
        mesh=mesh,
        in_specs=placed,
        out_specs=(P(("req", "seq"), None), P("req", "seq", None, None)),
        check_vma=False,
    )
```

```python
import jax
import jax.numpy as jnp
from jax import lax
from jax.sharding import PartitionSpec as P

N = 128
STRETCH = 256


def from_behind(value, axis, steps):
    count = lax.axis_size(axis)
    leading, last = (max(0, -steps), min(count, count - steps))
    return lax.ppermute(value, axis, [(source, source + steps) for source in range(leading, last)])


LMAX_CH = 16


def chain_flat(earlier, later):
    return (earlier[0] * later[0], later[0][:, None] * earlier[1] + later[1])


def carried_in(gain, state, window):
    groups = lax.axis_size("seq")
    heads = gain.shape[0]
    share = heads // groups
    cells = state.shape[1] * state.shape[2]
    packed = jnp.concatenate(
        [state.reshape(heads, cells), jnp.broadcast_to(gain[:, None], (heads, 128))], axis=1
    )
    mine = lax.all_to_all(packed, "seq", split_axis=0, concat_axis=0, tiled=True)
    mine = mine.reshape(groups, share, cells + 128)
    parts = [(mine[k, :, cells], mine[k, :, :cells]) for k in range(groups)]
    prefixes = [(jnp.ones((share,), jnp.float32), jnp.zeros((share, cells), jnp.float32))]
    for k in range(groups):
        prefixes.append(chain_flat(prefixes[-1], parts[k]))
    whole = prefixes[-1]
    reach = -(-window // groups)
    behind = from_behind(whole, "req", reach)
    for step in range(reach - 1, 0, -1):
        behind = chain_flat(behind, from_behind(whole, "req", step))
    incoming = jnp.stack([chain_flat(behind, prefixes[k])[1] for k in range(groups)], axis=0)
    incoming = lax.all_to_all(incoming, "seq", split_axis=0, concat_axis=0, tiled=True)
    return incoming.reshape(state.shape)


def stretch_flags(prompt_stretches, stretch_ids):
    firsts = jnp.cumsum(prompt_stretches) - prompt_stretches
    last_stretches = firsts + prompt_stretches - 1
    starts = jnp.any(stretch_ids[:, None] == firsts[None, :], axis=1)
    finals = jnp.any(stretch_ids[:, None] == last_stretches[None, :], axis=1)
    return (starts, finals)


def causal_conv(row_block, history, weight, conv_bias, starts):
    conv_span = weight.shape[0]
    length = row_block.shape[0]
    extended = jnp.concatenate([history, row_block], axis=0)
    in_stretch = jnp.arange(length, dtype=jnp.int32) % STRETCH
    start_rows = jnp.repeat(starts, STRETCH)
    running = conv_bias[None, :]
    for offset in range(conv_span):
        lag_rows = conv_span - 1 - offset
        shifted = extended[offset : offset + length].astype(jnp.float32)
        usable = jnp.logical_not((in_stretch < lag_rows) & start_rows)
        running = running + weight[offset][None, :] * jnp.where(usable[:, None], shifted, 0.0)
    return jax.nn.silu(running).astype(jnp.bfloat16)


def stretch_summary(x_stretch, bc_stretch, dt_stretch, dt_bias, a_log):
    state_size = bc_stretch.shape[1] // 2
    b_mat = bc_stretch[:, :state_size]
    step_size = jax.nn.softplus(dt_stretch.astype(jnp.float32) + dt_bias[None, :])
    log_decay = jnp.cumsum(-jnp.exp(a_log)[None, :] * step_size, axis=0)
    tail_weight = jnp.exp(log_decay[-1][None, :] - log_decay) * step_size
    weighted_x = (x_stretch.astype(jnp.float32) * tail_weight[:, :, None]).astype(jnp.bfloat16)
    stretch_state = jnp.einsum("uhp,un->hpn", weighted_x, b_mat, preferred_element_type=jnp.float32)
    return (step_size, log_decay, stretch_state)


def stretch_diag(x_stretch, bc_stretch, step_size, log_decay):
    state_size = bc_stretch.shape[1] // 2
    b_mat = bc_stretch[:, :state_size]
    c_mat = bc_stretch[:, state_size:]
    scores = jnp.dot(c_mat, b_mat.T, preferred_element_type=jnp.float32)
    stretch_len = scores.shape[0]
    causal = jnp.arange(stretch_len)[:, None] >= jnp.arange(stretch_len)[None, :]
    by_head = log_decay.T
    segment = by_head[:, :, None] - by_head[:, None, :]
    decay_mask = jnp.where(causal[None], jnp.exp(jnp.where(causal[None], segment, 0.0)), 0.0)
    mixing = (scores[None] * decay_mask * step_size.T[:, None, :]).astype(jnp.bfloat16)
    return jnp.einsum("htu,uhp->thp", mixing, x_stretch, preferred_element_type=jnp.float32)


def finish_stretch(y_diag, log_decay, state_in, x_stretch, c_mat, d_skip):
    state_low = state_in.astype(jnp.bfloat16)
    y_off = jnp.exp(log_decay)[:, :, None] * jnp.einsum(
        "tn,hpn->thp", c_mat, state_low, preferred_element_type=jnp.float32
    )
    mixed_rows = y_diag + y_off + d_skip[None, :, None] * x_stretch.astype(jnp.float32)
    return mixed_rows.reshape(mixed_rows.shape[0], -1).astype(jnp.bfloat16)


def gate_and_norm(mixed_rows, z_rows, norm_gain):
    gated_rows = mixed_rows.astype(jnp.float32) * jax.nn.silu(z_rows.astype(jnp.float32))
    inv_rms = lax.rsqrt(jnp.mean(gated_rows * gated_rows, axis=-1, keepdims=True) + 1e-05)
    return (gated_rows * inv_rms * norm_gain[None, :]).astype(jnp.bfloat16)


def chain_states(earlier, later):
    return (earlier[0] * later[0], later[0][:, None, None] * earlier[1] + later[1])


def per_device(
    x_in,
    bc_in,
    z_in,
    dt_raw,
    conv_weight,
    conv_bias,
    dt_bias,
    a_log,
    d_skip,
    norm_gain,
    w_out,
    prompt_stretches,
):
    n_req = lax.axis_size("req")
    n_seq = lax.axis_size("seq")
    tok_rows, inner_width = x_in.shape
    head_count = a_log.shape[0]
    head_dim = inner_width // head_count
    share = head_count // n_seq
    width = share * head_dim
    chunk = tok_rows // n_req
    bc_width = bc_in.shape[1]
    state_size = bc_width // 2
    conv_span = conv_weight.shape[0]
    group = lax.axis_index("seq")
    block = lax.axis_index("req")

    x_slabs = jnp.stack([x_in[:, g * width : (g + 1) * width] for g in range(n_seq)], axis=0)
    dt_slabs = jnp.stack([dt_raw[:, g * share : (g + 1) * share] for g in range(n_seq)], axis=0)
    bc_slabs = jnp.broadcast_to(bc_in[None], (n_seq, tok_rows, bc_width))
    outbound = jnp.concatenate([x_slabs, bc_slabs, dt_slabs], axis=2)
    outbound = outbound.reshape(n_seq * n_req, chunk, -1)
    inbound = lax.all_to_all(outbound, ("seq", "req"), 0, 0, tiled=True)
    inbound = inbound.reshape(n_seq * tok_rows, -1)
    x_rows = inbound[:, :width]
    bc_rows = inbound[:, width : width + bc_width]
    dt_rows = inbound[:, width + bc_width :]

    row_count = x_rows.shape[0]
    stretch_count = row_count // STRETCH
    stretch_ids = block * stretch_count + jnp.arange(stretch_count, dtype=jnp.int32)
    starts, finals = stretch_flags(prompt_stretches, stretch_ids)
    edge = from_behind(inbound[row_count - conv_span + 1 :, : width + bc_width], "req", 1)
    edge_x = edge[:, :width]
    edge_bc = edge[:, width:]
    weight_x = lax.dynamic_slice_in_dim(conv_weight, group * width, width, axis=1)
    bias_x = lax.dynamic_slice_in_dim(conv_bias, group * width, width, axis=0)
    conv_x = causal_conv(x_rows, edge_x, weight_x, bias_x, starts)
    conv_bc = causal_conv(
        bc_rows, edge_bc, conv_weight[:, inner_width:], conv_bias[inner_width:], starts
    )
    bias_dt = lax.dynamic_slice_in_dim(dt_bias, group * share, share)
    rate_log = lax.dynamic_slice_in_dim(a_log, group * share, share)
    skip = lax.dynamic_slice_in_dim(d_skip, group * share, share)

    x_heads = conv_x.reshape(stretch_count, STRETCH, share, head_dim)
    bcs = conv_bc.reshape(stretch_count, STRETCH, bc_width)
    b_mat = bcs[:, :, :state_size]
    c_mat = bcs[:, :, state_size:]
    dts = dt_rows.reshape(stretch_count, STRETCH, share)
    step_size = jax.nn.softplus(dts.astype(jnp.float32) + bias_dt[None, None, :])
    rates = -jnp.exp(rate_log)[None, None, :] * step_size
    lower = (jnp.arange(STRETCH)[:, None] >= jnp.arange(STRETCH)[None, :]).astype(jnp.float32)
    log_decay = jnp.einsum(
        "tu,cuh->cth", lower, rates, precision=lax.Precision.HIGHEST,
        preferred_element_type=jnp.float32,
    )
    tail_weight = jnp.exp(log_decay[:, -1:, :] - log_decay) * step_size
    weighted_x = (
        x_heads.astype(jnp.float32) * tail_weight[..., None]
    ).astype(jnp.bfloat16).reshape(stretch_count, STRETCH, width)
    stretch_state = jnp.einsum(
        "cun,cuq->cnq", b_mat, weighted_x, preferred_element_type=jnp.float32
    )
    carried = jnp.repeat(
        jnp.where(starts[:, None], 0.0, jnp.exp(log_decay[:, -1, :])), head_dim, axis=-1
    )

    def chain_cols(earlier, later):
        return (earlier[0] * later[0], later[0][None, :] * earlier[1] + later[1])

    total = (jnp.ones((width,), jnp.float32), jnp.zeros((N, width), jnp.float32))
    for stretch in range(stretch_count):
        total = chain_cols(total, (carried[stretch], stretch_state[stretch]))
    reach = -(-(LMAX_CH - 1) // stretch_count)
    packed = jnp.concatenate([total[1], total[0][None, :]], axis=0)

    def unpack(moved):
        return (moved[N], moved[:N])

    behind = unpack(from_behind(packed, "req", reach))
    for step in range(reach - 1, 0, -1):
        behind = chain_cols(behind, unpack(from_behind(packed, "req", step)))
    state_prev = behind[1]

    scores = jnp.einsum("ctn,cun->ctu", c_mat, b_mat, preferred_element_type=jnp.float32)
    causal = jnp.arange(STRETCH)[:, None] >= jnp.arange(STRETCH)[None, :]
    by_head = log_decay.transpose(0, 2, 1)
    segment = by_head[:, :, :, None] - by_head[:, :, None, :]
    decay_mask = jnp.where(causal, jnp.exp(jnp.where(causal, segment, 0.0)), 0.0)
    mixing = (
        scores[:, None] * decay_mask * step_size.transpose(0, 2, 1)[:, :, None, :]
    ).astype(jnp.bfloat16)

    keep = jnp.where(starts, 0.0, 1.0)
    gains = jnp.exp(log_decay[:, -1, :])
    c_idx = jnp.arange(stretch_count)[:, None, None]
    k_idx = jnp.arange(-1, stretch_count)[None, :, None]
    m_idx = jnp.arange(stretch_count)[None, None, :]
    keep_span = (m_idx > k_idx) & (m_idx <= c_idx)
    gain_span = (m_idx > k_idx) & (m_idx < c_idx)
    live = k_idx < c_idx
    factors = jnp.where(keep_span[..., None], keep[None, None, :, None], 1.0) * jnp.where(
        gain_span[..., None], gains[None, None, :, :], 1.0
    )
    weights = jnp.where(live, jnp.prod(factors, axis=2), 0.0)
    sources = jnp.concatenate([state_prev[None], stretch_state], axis=0)
    weights = jnp.repeat(weights, head_dim, axis=-1)
    state_in_all = jnp.sum(weights[:, :, None, :] * sources[None], axis=1)
    gains_cols = jnp.repeat(gains, head_dim, axis=-1)
    state_out_all = gains_cols[:, None, :] * state_in_all + stretch_state
    endings = jnp.where(finals[:, None, None], state_out_all, 0.0)
    endings = endings.reshape(stretch_count, N, share, head_dim).transpose(0, 2, 3, 1)
    state_low = state_in_all.astype(jnp.bfloat16)
    y_off = jnp.repeat(jnp.exp(log_decay), head_dim, axis=-1) * jnp.einsum(
        "ctn,cnq->ctq", c_mat, state_low, preferred_element_type=jnp.float32
    )
    y_diag = jnp.concatenate(
        [
            jnp.einsum(
                "ctu,cup->ctp", mixing[:, h], x_heads[:, :, h], preferred_element_type=jnp.float32
            )
            for h in range(share)
        ],
        axis=-1,
    )
    x_flat = conv_x.reshape(stretch_count, STRETCH, width).astype(jnp.float32)
    mixed = y_diag + y_off + jnp.repeat(skip, head_dim)[None, None, :] * x_flat
    mixed = mixed.astype(jnp.bfloat16).reshape(n_seq * n_req, chunk, width)
    back = lax.all_to_all(mixed, ("seq", "req"), 0, 0, tiled=True)
    back = back.reshape(n_seq, tok_rows, width)
    mixed_tokens = jnp.concatenate([back[g] for g in range(n_seq)], axis=1)
    normed = gate_and_norm(mixed_tokens, z_in, norm_gain)
    mixed_out = jnp.dot(normed, w_out, preferred_element_type=jnp.float32).astype(jnp.bfloat16)
    return (mixed_out, endings)


def solution(mesh):
    placed = (
        P(("req", "seq"), None),
        P(("req", "seq"), None),
        P(("req", "seq"), None),
        P(("req", "seq"), None),
        P(),
        P(),
        P(),
        P(),
        P(),
        P(),
        P(),
        P(),
    )
    return jax.shard_map(
        per_device,
        mesh=mesh,
        in_specs=placed,
        out_specs=(P(("req", "seq"), None), P("req", "seq", None, None)),
        check_vma=False,
    )
```

```python
import jax
import jax.numpy as jnp
from jax import lax
from jax.sharding import PartitionSpec as P

N = 128
STRETCH = 256


def from_behind(value, axis, steps):
    count = lax.axis_size(axis)
    leading, last = (max(0, -steps), min(count, count - steps))
    return lax.ppermute(value, axis, [(source, source + steps) for source in range(leading, last)])


LMAX_CH = 16


def chain_flat(earlier, later):
    return (earlier[0] * later[0], later[0][:, None] * earlier[1] + later[1])


def carried_in(gain, state, window):
    groups = lax.axis_size("seq")
    heads = gain.shape[0]
    share = heads // groups
    cells = state.shape[1] * state.shape[2]
    packed = jnp.concatenate(
        [state.reshape(heads, cells), jnp.broadcast_to(gain[:, None], (heads, 128))], axis=1
    )
    mine = lax.all_to_all(packed, "seq", split_axis=0, concat_axis=0, tiled=True)
    mine = mine.reshape(groups, share, cells + 128)
    parts = [(mine[k, :, cells], mine[k, :, :cells]) for k in range(groups)]
    prefixes = [(jnp.ones((share,), jnp.float32), jnp.zeros((share, cells), jnp.float32))]
    for k in range(groups):
        prefixes.append(chain_flat(prefixes[-1], parts[k]))
    whole = prefixes[-1]
    reach = -(-window // groups)
    behind = from_behind(whole, "req", reach)
    for step in range(reach - 1, 0, -1):
        behind = chain_flat(behind, from_behind(whole, "req", step))
    incoming = jnp.stack([chain_flat(behind, prefixes[k])[1] for k in range(groups)], axis=0)
    incoming = lax.all_to_all(incoming, "seq", split_axis=0, concat_axis=0, tiled=True)
    return incoming.reshape(state.shape)


def stretch_flags(prompt_stretches, stretch_ids):
    firsts = jnp.cumsum(prompt_stretches) - prompt_stretches
    last_stretches = firsts + prompt_stretches - 1
    starts = jnp.any(stretch_ids[:, None] == firsts[None, :], axis=1)
    finals = jnp.any(stretch_ids[:, None] == last_stretches[None, :], axis=1)
    return (starts, finals)


def causal_conv(row_block, history, weight, conv_bias, starts):
    conv_span = weight.shape[0]
    length = row_block.shape[0]
    extended = jnp.concatenate([history, row_block], axis=0)
    in_stretch = jnp.arange(length, dtype=jnp.int32) % STRETCH
    start_rows = jnp.repeat(starts, STRETCH)
    running = conv_bias[None, :]
    for offset in range(conv_span):
        lag_rows = conv_span - 1 - offset
        shifted = extended[offset : offset + length].astype(jnp.float32)
        usable = jnp.logical_not((in_stretch < lag_rows) & start_rows)
        running = running + weight[offset][None, :] * jnp.where(usable[:, None], shifted, 0.0)
    return jax.nn.silu(running).astype(jnp.bfloat16)


def stretch_summary(x_stretch, bc_stretch, dt_stretch, dt_bias, a_log):
    state_size = bc_stretch.shape[1] // 2
    b_mat = bc_stretch[:, :state_size]
    step_size = jax.nn.softplus(dt_stretch.astype(jnp.float32) + dt_bias[None, :])
    log_decay = jnp.cumsum(-jnp.exp(a_log)[None, :] * step_size, axis=0)
    tail_weight = jnp.exp(log_decay[-1][None, :] - log_decay) * step_size
    weighted_x = (x_stretch.astype(jnp.float32) * tail_weight[:, :, None]).astype(jnp.bfloat16)
    stretch_state = jnp.einsum("uhp,un->hpn", weighted_x, b_mat, preferred_element_type=jnp.float32)
    return (step_size, log_decay, stretch_state)


def stretch_diag(x_stretch, bc_stretch, step_size, log_decay):
    state_size = bc_stretch.shape[1] // 2
    b_mat = bc_stretch[:, :state_size]
    c_mat = bc_stretch[:, state_size:]
    scores = jnp.dot(c_mat, b_mat.T, preferred_element_type=jnp.float32)
    stretch_len = scores.shape[0]
    causal = jnp.arange(stretch_len)[:, None] >= jnp.arange(stretch_len)[None, :]
    by_head = log_decay.T
    segment = by_head[:, :, None] - by_head[:, None, :]
    decay_mask = jnp.where(causal[None], jnp.exp(jnp.where(causal[None], segment, 0.0)), 0.0)
    mixing = (scores[None] * decay_mask * step_size.T[:, None, :]).astype(jnp.bfloat16)
    return jnp.einsum("htu,uhp->thp", mixing, x_stretch, preferred_element_type=jnp.float32)


def finish_stretch(y_diag, log_decay, state_in, x_stretch, c_mat, d_skip):
    state_low = state_in.astype(jnp.bfloat16)
    y_off = jnp.exp(log_decay)[:, :, None] * jnp.einsum(
        "tn,hpn->thp", c_mat, state_low, preferred_element_type=jnp.float32
    )
    mixed_rows = y_diag + y_off + d_skip[None, :, None] * x_stretch.astype(jnp.float32)
    return mixed_rows.reshape(mixed_rows.shape[0], -1).astype(jnp.bfloat16)


def gate_and_norm(mixed_rows, z_rows, norm_gain):
    gated_rows = mixed_rows.astype(jnp.float32) * jax.nn.silu(z_rows.astype(jnp.float32))
    inv_rms = lax.rsqrt(jnp.mean(gated_rows * gated_rows, axis=-1, keepdims=True) + 1e-05)
    return (gated_rows * inv_rms * norm_gain[None, :]).astype(jnp.bfloat16)


def chain_states(earlier, later):
    return (earlier[0] * later[0], later[0][:, None, None] * earlier[1] + later[1])


def per_device(
    x_in,
    bc_in,
    z_in,
    dt_raw,
    conv_weight,
    conv_bias,
    dt_bias,
    a_log,
    d_skip,
    norm_gain,
    w_out,
    prompt_stretches,
):
    n_req = lax.axis_size("req")
    n_seq = lax.axis_size("seq")
    tok_rows, inner_width = x_in.shape
    head_count = a_log.shape[0]
    head_dim = inner_width // head_count
    share = head_count // n_seq
    width = share * head_dim
    chunk = tok_rows // n_req
    bc_width = bc_in.shape[1]
    state_size = bc_width // 2
    conv_span = conv_weight.shape[0]
    group = lax.axis_index("seq")
    block = lax.axis_index("req")

    x_slabs = jnp.stack([x_in[:, g * width : (g + 1) * width] for g in range(n_seq)], axis=0)
    bc_slabs = jnp.broadcast_to(bc_in[None], (n_seq, tok_rows, bc_width))
    outbound = jnp.concatenate([x_slabs, bc_slabs], axis=2)
    dt_chunks = dt_raw.reshape(n_req, chunk, n_seq, share).transpose(2, 0, 1, 3)
    dt_chunks = dt_chunks.reshape(n_seq * n_req, chunk * share)
    dt_rows = lax.all_to_all(dt_chunks, ("seq", "req"), 0, 0, tiled=True)
    dt_rows = dt_rows.reshape(n_seq * tok_rows, share)
    outbound = outbound.reshape(n_seq * n_req, chunk, -1)
    inbound = lax.all_to_all(outbound, ("seq", "req"), 0, 0, tiled=True)
    inbound = inbound.reshape(n_seq * tok_rows, -1)
    x_rows = inbound[:, :width]
    bc_rows = inbound[:, width : width + bc_width]

    row_count = x_rows.shape[0]
    stretch_count = row_count // STRETCH
    stretch_ids = block * stretch_count + jnp.arange(stretch_count, dtype=jnp.int32)
    starts, finals = stretch_flags(prompt_stretches, stretch_ids)
    edge = from_behind(inbound[row_count - conv_span + 1 :, : width + bc_width], "req", 1)
    edge_x = edge[:, :width]
    edge_bc = edge[:, width:]
    weight_x = lax.dynamic_slice_in_dim(conv_weight, group * width, width, axis=1)
    bias_x = lax.dynamic_slice_in_dim(conv_bias, group * width, width, axis=0)
    conv_x = causal_conv(x_rows, edge_x, weight_x, bias_x, starts)
    conv_bc = causal_conv(
        bc_rows, edge_bc, conv_weight[:, inner_width:], conv_bias[inner_width:], starts
    )
    bias_dt = lax.dynamic_slice_in_dim(dt_bias, group * share, share)
    rate_log = lax.dynamic_slice_in_dim(a_log, group * share, share)
    skip = lax.dynamic_slice_in_dim(d_skip, group * share, share)

    x_heads = conv_x.reshape(stretch_count, STRETCH, share, head_dim)
    bcs = conv_bc.reshape(stretch_count, STRETCH, bc_width)
    b_mat = bcs[:, :, :state_size]
    c_mat = bcs[:, :, state_size:]
    dts = dt_rows.reshape(stretch_count, STRETCH, share)
    step_size = jax.nn.softplus(dts.astype(jnp.float32) + bias_dt[None, None, :])
    rates = -jnp.exp(rate_log)[None, None, :] * step_size
    lower = (jnp.arange(STRETCH)[:, None] >= jnp.arange(STRETCH)[None, :]).astype(jnp.float32)
    log_decay = jnp.einsum(
        "tu,cuh->cth", lower, rates, precision=lax.Precision.HIGHEST,
        preferred_element_type=jnp.float32,
    )
    tail_weight = jnp.exp(log_decay[:, -1:, :] - log_decay) * step_size
    weighted_x = (x_heads.astype(jnp.float32) * tail_weight[..., None]).astype(jnp.bfloat16)
    stretch_state = jnp.einsum(
        "cuhp,cun->chpn", weighted_x, b_mat, preferred_element_type=jnp.float32
    )
    carried = jnp.where(starts[:, None], 0.0, jnp.exp(log_decay[:, -1, :]))
    total = (jnp.ones((share,), jnp.float32), jnp.zeros((share, head_dim, N), jnp.float32))
    for stretch in range(stretch_count):
        total = chain_states(total, (carried[stretch], stretch_state[stretch]))
    reach = -(-(LMAX_CH - 1) // stretch_count)
    cells = head_dim * N
    packed = jnp.concatenate(
        [total[1].reshape(share, cells), jnp.broadcast_to(total[0][:, None], (share, 128))],
        axis=1,
    )

    def unpack(moved):
        return (moved[:, cells], moved[:, :cells].reshape(share, head_dim, N))

    behind = unpack(from_behind(packed, "req", reach))
    for step in range(reach - 1, 0, -1):
        behind = chain_states(behind, unpack(from_behind(packed, "req", step)))
    state_prev = behind[1]

    scores = jnp.einsum("ctn,cun->ctu", c_mat, b_mat, preferred_element_type=jnp.float32)
    causal = jnp.arange(STRETCH)[:, None] >= jnp.arange(STRETCH)[None, :]
    by_head = log_decay.transpose(0, 2, 1)
    segment = by_head[:, :, :, None] - by_head[:, :, None, :]
    decay_mask = jnp.where(causal, jnp.exp(jnp.where(causal, segment, 0.0)), 0.0)
    mixing = (
        scores[:, None] * decay_mask * step_size.transpose(0, 2, 1)[:, :, None, :]
    ).astype(jnp.bfloat16)

    keep = jnp.where(starts, 0.0, 1.0)
    gains = jnp.exp(log_decay[:, -1, :])
    c_idx = jnp.arange(stretch_count)[:, None, None]
    k_idx = jnp.arange(-1, stretch_count)[None, :, None]
    m_idx = jnp.arange(stretch_count)[None, None, :]
    keep_span = (m_idx > k_idx) & (m_idx <= c_idx)
    gain_span = (m_idx > k_idx) & (m_idx < c_idx)
    live = k_idx < c_idx
    factors = jnp.where(keep_span[..., None], keep[None, None, :, None], 1.0) * jnp.where(
        gain_span[..., None], gains[None, None, :, :], 1.0
    )
    weights = jnp.where(live, jnp.prod(factors, axis=2), 0.0)
    sources = jnp.concatenate([state_prev[None], stretch_state], axis=0)
    state_in_all = jnp.sum(weights[:, :, :, None, None] * sources[None], axis=1)
    state_out_all = gains[:, :, None, None] * state_in_all + stretch_state
    endings = jnp.where(finals[:, None, None, None], state_out_all, 0.0)
    state_ins = [state_in_all[c] for c in range(stretch_count)]
    state_low = jnp.stack(state_ins, axis=0).astype(jnp.bfloat16)
    state_low = state_low.reshape(stretch_count, width, N)
    y_off = jnp.repeat(jnp.exp(log_decay), head_dim, axis=-1) * jnp.einsum(
        "ctn,cqn->ctq", c_mat, state_low, preferred_element_type=jnp.float32
    )
    y_diag = jnp.concatenate(
        [
            jnp.einsum(
                "ctu,cup->ctp", mixing[:, h], x_heads[:, :, h], preferred_element_type=jnp.float32
            )
            for h in range(share)
        ],
        axis=-1,
    )
    x_flat = conv_x.reshape(stretch_count, STRETCH, width).astype(jnp.float32)
    mixed = y_diag + y_off + jnp.repeat(skip, head_dim)[None, None, :] * x_flat
    mixed = mixed.astype(jnp.bfloat16).reshape(n_seq * n_req, chunk, width)
    back = lax.all_to_all(mixed, ("seq", "req"), 0, 0, tiled=True)
    back = back.reshape(n_seq, tok_rows, width)
    mixed_tokens = jnp.concatenate([back[g] for g in range(n_seq)], axis=1)
    normed = gate_and_norm(mixed_tokens, z_in, norm_gain)
    mixed_out = jnp.dot(normed, w_out, preferred_element_type=jnp.float32).astype(jnp.bfloat16)
    return (mixed_out, endings)


def solution(mesh):
    placed = (
        P(("req", "seq"), None),
        P(("req", "seq"), None),
        P(("req", "seq"), None),
        P(("req", "seq"), None),
        P(),
        P(),
        P(),
        P(),
        P(),
        P(),
        P(),
        P(),
    )
    return jax.shard_map(
        per_device,
        mesh=mesh,
        in_specs=placed,
        out_specs=(P(("req", "seq"), None), P("req", "seq", None, None)),
        check_vma=False,
    )
```
